32 devices in a mesh: year: 8 (over z, x), region: 4 (over y, core).
Axes of the slice: x: 2, y: 2, z: 4, core: 2. Of those that a mesh axis runs over, the one named last changes fastest.
Arguments:
- daily_temps: bfloat16 [8, 22, 512], P('year', None, 'region'), may hold values from -6 to 6
- land_mask: int32 [512], P('region'), may hold values 0 or 1
Outputs:
- coarse_threshold: float32 [8, 512], P('year', 'region')
- refined_threshold: float32 [8, 512], P('year', 'region')
The draws below stay inside these ranges and needn't reach their ends.
All inputs are finite; a program needn't handle non-finite values. No bound on the sum of `land_mask` on one device may be relied on, other than what follows from the above.
Results may differ from the reference program's by a relative error of at most 0.0013.
Values may be sent and summed in bfloat16 or wider, within the bound.
No kernel may reach another device: no remote copies, remote signals or barrier semaphores. Data moves between devices by JAX's collectives and lax.ppermute only.
A program may use at most 64 MiB of HBM per device.

```python
import jax
import jax.numpy as jnp
from jax import lax

WIN = 15
BINS = 256
YEARS = 8
DAYS_IN = 22
LON = 512


def with_ends(drawn, own_key, least, largest):
    spot = [jax.random.randint(jax.random.fold_in(own_key, axis), (), 0, length) for axis, length in enumerate(drawn.shape)]
    widest = drawn.shape.index(max(drawn.shape))
    next_to = spot[:widest] + [(spot[widest] + 1) % drawn.shape[widest]] + spot[widest + 1:]
    return drawn.at[tuple(spot)].set(least).at[tuple(next_to)].set(largest)


def levels(stream_key, shape, split, low, largest):
    level = 1.0
    for dim, parts in split:
        draws = jax.random.uniform(jax.random.fold_in(jax.random.fold_in(stream_key, 6), dim), (parts,), jnp.float32, low / len(split), largest / len(split))
        level = level * jnp.repeat(jnp.exp(draws), shape[dim] // parts).reshape((-1,) + (1,) * (len(shape) - 1 - dim))
    return level


def noise(own_key, dims, scale, bound, pieces=(), held_as=jnp.bfloat16):
    values = jax.random.normal(own_key, dims, jnp.float32) * scale
    if len(pieces) > 0:
        values = levels(own_key, dims, pieces, -0.22, 0.18) * values
    return jnp.clip(values, min=-bound, max=bound).astype(held_as)


def setup_inputs(seed: int = 0) -> dict:
    key_list = jax.random.split(jax.random.key(seed), 3)
    return {
        "daily_temps": noise(key_list[0], (YEARS, DAYS_IN, LON), 1.5, 6.0, ((0, 8), (2, 4))),
        "land_mask": with_ends((jax.random.randint(key_list[1], (LON,), 0, 3) < 1).astype(jnp.int32), jax.random.fold_in(key_list[1], 1), 0, 1),
    }


VALUE_RANGE = 12.8
QUANT_LEVEL = 0.9
SHARPNESS = 32.0
KERNEL_SCALE = 0.25
STEP_SIZE = 2.0


def smooth_field(extended, flags):
    center = extended[..., 1:-1]
    same_west = 1.0 - jnp.abs(flags[1:-1] - flags[:-2])
    same_east = 1.0 - jnp.abs(flags[1:-1] - flags[2:])
    mixed = center + same_west * extended[..., :-2] + same_east * extended[..., 2:]
    return (mixed / (1.0 + same_west + same_east)).astype(jnp.bfloat16)


def bin_weights(year_field, bin_count):
    width = VALUE_RANGE / bin_count
    scaled = jnp.clip((year_field.astype(jnp.float32) + 0.5 * VALUE_RANGE) / width, 0.0, bin_count - 1.0)
    centers = jnp.arange(bin_count, dtype=jnp.float32)
    return jnp.maximum(0.0, 1.0 - jnp.abs(scaled[..., None] - centers)).astype(jnp.bfloat16)


def quantile(histogram, count_all, bin_count):
    width = VALUE_RANGE / bin_count
    cumulative = jnp.cumsum(histogram, axis=-1)
    ranks = jnp.clip(0.5 + SHARPNESS * (QUANT_LEVEL - cumulative / count_all), 0.0, 1.0)
    return -0.5 * VALUE_RANGE + width * jnp.sum(ranks, axis=-1)


def day_band(first_row, row_count, days_in):
    row_day = first_row + lax.broadcasted_iota(jnp.int32, (row_count, days_in), 0)
    column_day = lax.broadcasted_iota(jnp.int32, (row_count, days_in), 1)
    inside = (column_day >= row_day) & (column_day < row_day + WIN)
    return jnp.where(inside, 1.0, 0.0).astype(jnp.bfloat16)


def window_cdf(threshold, year_field):
    cal_days = threshold.shape[0]
    samples = year_field.astype(jnp.float32)
    running = jnp.zeros(threshold.shape, jnp.float32)
    for offset in range(WIN):
        window = samples[:, offset:offset + cal_days, :]
        running = running + jnp.sum(jax.nn.sigmoid((threshold[None] - window) / KERNEL_SCALE), axis=0)
    return running


def reference(daily_temps, land_mask):
    years, days_in, lon_cells = daily_temps.shape
    cal_days = days_in - WIN + 1
    flags = land_mask.astype(jnp.float32)
    samples = daily_temps.astype(jnp.float32)
    extended = jnp.concatenate([samples[..., -1:], samples, samples[..., :1]], axis=-1)
    flag_ext = jnp.concatenate([flags[-1:], flags, flags[:1]])
    smoothed = smooth_field(extended, flag_ext)
    day_rows = day_band(0, cal_days, days_in)

    def add_year(running, year_field):
        weights = bin_weights(year_field, BINS).reshape(days_in, lon_cells * BINS)
        return running + jnp.dot(day_rows, weights, preferred_element_type=jnp.float32), None

    histogram, unused = lax.scan(add_year, jnp.zeros((cal_days, lon_cells * BINS), jnp.float32), smoothed)
    count_all = float(years * WIN)
    coarse = quantile(histogram.reshape(cal_days, lon_cells, BINS), count_all, BINS)
    cdf_sums = window_cdf(coarse, smoothed)
    refined = coarse - STEP_SIZE * (cdf_sums / count_all - QUANT_LEVEL)
    return coarse, refined
```

```python
import jax
import jax.numpy as jnp
from jax import lax
from jax.sharding import PartitionSpec as P

WIN = 15
BINS = 256


VALUE_RANGE = 12.8
QUANT_LEVEL = 0.9
SHARPNESS = 32.0
KERNEL_SCALE = 0.25
STEP_SIZE = 2.0


def extended_2(array, sides, width):
    for axis, dim in sides:
        devices, length = (lax.axis_size(axis), array.shape[dim])
        up = [(i, (i + 1) % devices) for i in range(devices)]
        down = [(j, i) for i, j in up]
        last = lax.slice_in_dim(array, length - width, length, axis=dim)
        leading = lax.slice_in_dim(array, 0, width, axis=dim)
        before = lax.ppermute(last, axis, up)
        after = lax.ppermute(leading, axis, down)
        array = jnp.concatenate([before, array, after], axis=dim)
    return array


def smooth_field(extended, flags):
    center = extended[..., 1:-1]
    same_west = 1.0 - jnp.abs(flags[1:-1] - flags[:-2])
    same_east = 1.0 - jnp.abs(flags[1:-1] - flags[2:])
    mixed = center + same_west * extended[..., :-2] + same_east * extended[..., 2:]
    return (mixed / (1.0 + same_west + same_east)).astype(jnp.bfloat16)


def gather_years(block, axis):
    devices = lax.axis_size(axis)
    pieces = [block]
    for shift in range(1, devices):
        pairs = [(i, (i + shift) % devices) for i in range(devices)]
        pieces.append(lax.ppermute(block, axis, pairs))
    return jnp.stack(pieces, axis=0)


def coarse_from_samples(samples, count_all, bin_count):
    width = VALUE_RANGE / bin_count
    scaled = jnp.clip((samples + 0.5 * VALUE_RANGE) / width, 0.0, bin_count - 1.0)
    upper = lax.broadcasted_iota(jnp.float32, (bin_count, 1), 0) + 1.0
    cumulative = jnp.sum(jnp.clip(upper[None] - scaled[:, None, :], 0.0, 1.0), axis=0)
    ranks = jnp.clip(0.5 + SHARPNESS * (QUANT_LEVEL - cumulative / count_all), 0.0, 1.0)
    return -0.5 * VALUE_RANGE + width * jnp.sum(ranks, axis=0)


def shards(daily_temps, land_mask):
    days_in = daily_temps.shape[1]
    year_count = lax.axis_size("year")
    cal_days = days_in - WIN + 1
    cal_own = cal_days // year_count
    count_all = float(year_count * WIN)
    flag_row = land_mask.astype(jnp.bfloat16)[None, :]
    stacked = jnp.concatenate([daily_temps[0], flag_row], axis=0)
    extended = extended_2(stacked, (("region", 1),), 1)
    smoothed = smooth_field(
        extended[:days_in].astype(jnp.float32), extended[days_in].astype(jnp.float32)
    )
    every_year = gather_years(smoothed, "year").astype(jnp.float32)
    first_day = lax.axis_index("year") * cal_own
    coarse_rows = []
    refined_rows = []
    for j in range(cal_own):
        window = lax.dynamic_slice_in_dim(every_year, first_day + j, WIN, axis=1)
        samples = window.reshape(-1, window.shape[-1])
        coarse = coarse_from_samples(samples, count_all, BINS)
        cdf = jnp.sum(jax.nn.sigmoid((coarse[None] - samples) / KERNEL_SCALE), axis=0)
        refined = coarse - STEP_SIZE * (cdf / count_all - QUANT_LEVEL)
        coarse_rows.append(coarse)
        refined_rows.append(refined)
    return (jnp.stack(coarse_rows, axis=0), jnp.stack(refined_rows, axis=0))


def solution(mesh):
    return jax.shard_map(
        shards,
        mesh=mesh,
        in_specs=(P("year", None, "region"), P("region")),
        out_specs=(P("year", "region"), P("year", "region")),
        check_vma=False,
    )
```

```python
import jax
import jax.numpy as jnp
from jax import lax
from jax.sharding import PartitionSpec as P

WIN = 15
BINS = 256


VALUE_RANGE = 12.8
QUANT_LEVEL = 0.9
SHARPNESS = 32.0
KERNEL_SCALE = 0.25
STEP_SIZE = 2.0


def extended_2(array, sides, width):
    for axis, dim in sides:
        devices, length = (lax.axis_size(axis), array.shape[dim])
        up = [(i, (i + 1) % devices) for i in range(devices)]
        down = [(j, i) for i, j in up]
        last = lax.slice_in_dim(array, length - width, length, axis=dim)
        leading = lax.slice_in_dim(array, 0, width, axis=dim)
        before = lax.ppermute(last, axis, up)
        after = lax.ppermute(leading, axis, down)
        array = jnp.concatenate([before, array, after], axis=dim)
    return array


def smooth_field(extended, flags):
    center = extended[..., 1:-1]
    same_west = 1.0 - jnp.abs(flags[1:-1] - flags[:-2])
    same_east = 1.0 - jnp.abs(flags[1:-1] - flags[2:])
    mixed = center + same_west * extended[..., :-2] + same_east * extended[..., 2:]
    return (mixed / (1.0 + same_west + same_east)).astype(jnp.bfloat16)


def gather_years(block, axis):
    devices = lax.axis_size(axis)
    tiled = jnp.broadcast_to(block[None], (devices,) + block.shape)
    return lax.all_to_all(tiled, axis, 0, 0, tiled=True)


def coarse_from_samples(samples, count_all, bin_count):
    width = VALUE_RANGE / bin_count
    scaled = jnp.clip((samples + 0.5 * VALUE_RANGE) / width, 0.0, bin_count - 1.0)
    upper = lax.broadcasted_iota(jnp.float32, (bin_count, 1), 0) + 1.0
    cumulative = jnp.sum(jnp.clip(upper[None] - scaled[:, None, :], 0.0, 1.0), axis=0)
    ranks = jnp.clip(0.5 + SHARPNESS * (QUANT_LEVEL - cumulative / count_all), 0.0, 1.0)
    return -0.5 * VALUE_RANGE + width * jnp.sum(ranks, axis=0)


def shards(daily_temps, land_mask):
    days_in = daily_temps.shape[1]
    year_count = lax.axis_size("year")
    cal_days = days_in - WIN + 1
    cal_own = cal_days // year_count
    count_all = float(year_count * WIN)
    flag_row = land_mask.astype(jnp.bfloat16)[None, :]
    stacked = jnp.concatenate([daily_temps[0], flag_row], axis=0)
    extended = extended_2(stacked, (("region", 1),), 1)
    smoothed = smooth_field(
        extended[:days_in].astype(jnp.float32), extended[days_in].astype(jnp.float32)
    )
    every_year = gather_years(smoothed, "year").astype(jnp.float32)
    first_day = lax.axis_index("year") * cal_own
    coarse_rows = []
    refined_rows = []
    for j in range(cal_own):
        window = lax.dynamic_slice_in_dim(every_year, first_day + j, WIN, axis=1)
        samples = window.reshape(-1, window.shape[-1])
        coarse = coarse_from_samples(samples, count_all, BINS)
        cdf = jnp.sum(jax.nn.sigmoid((coarse[None] - samples) / KERNEL_SCALE), axis=0)
        refined = coarse - STEP_SIZE * (cdf / count_all - QUANT_LEVEL)
        coarse_rows.append(coarse)
        refined_rows.append(refined)
    return (jnp.stack(coarse_rows, axis=0), jnp.stack(refined_rows, axis=0))


def solution(mesh):
    return jax.shard_map(
        shards,
        mesh=mesh,
        in_specs=(P("year", None, "region"), P("region")),
        out_specs=(P("year", "region"), P("year", "region")),
        check_vma=False,
    )
```

```python
import jax
import jax.numpy as jnp
from jax import lax
from jax.sharding import PartitionSpec as P

WIN = 15
BINS = 256


VALUE_RANGE = 12.8
QUANT_LEVEL = 0.9
SHARPNESS = 32.0
KERNEL_SCALE = 0.25
STEP_SIZE = 2.0


def extended_2(array, sides, width):
    for axis, dim in sides:
        devices, length = (lax.axis_size(axis), array.shape[dim])
        up = [(i, (i + 1) % devices) for i in range(devices)]
        down = [(j, i) for i, j in up]
        last = lax.slice_in_dim(array, length - width, length, axis=dim)
        leading = lax.slice_in_dim(array, 0, width, axis=dim)
        before = lax.ppermute(last, axis, up)
        after = lax.ppermute(leading, axis, down)
        array = jnp.concatenate([before, array, after], axis=dim)
    return array


def smooth_field(extended, flags):
    center = extended[..., 1:-1]
    same_west = 1.0 - jnp.abs(flags[1:-1] - flags[:-2])
    same_east = 1.0 - jnp.abs(flags[1:-1] - flags[2:])
    mixed = center + same_west * extended[..., :-2] + same_east * extended[..., 2:]
    return (mixed / (1.0 + same_west + same_east)).astype(jnp.bfloat16)


def gather_years(block, axis):
    devices = lax.axis_size(axis)
    held = block[None]
    have = 1
    while have < devices:
        take = min(have, devices - have)
        pairs = [(i, (i + have) % devices) for i in range(devices)]
        held = jnp.concatenate([held, lax.ppermute(held[:take], axis, pairs)], axis=0)
        have += take
    return held


def coarse_from_samples(samples, count_all, bin_count):
    width = VALUE_RANGE / bin_count
    scaled = jnp.clip((samples + 0.5 * VALUE_RANGE) / width, 0.0, bin_count - 1.0)
    upper = lax.broadcasted_iota(jnp.float32, (bin_count, 1), 0) + 1.0
    cumulative = jnp.sum(jnp.clip(upper[None] - scaled[:, None, :], 0.0, 1.0), axis=0)
    ranks = jnp.clip(0.5 + SHARPNESS * (QUANT_LEVEL - cumulative / count_all), 0.0, 1.0)
    return -0.5 * VALUE_RANGE + width * jnp.sum(ranks, axis=0)


def shards(daily_temps, land_mask):
    days_in = daily_temps.shape[1]
    year_count = lax.axis_size("year")
    cal_days = days_in - WIN + 1
    cal_own = cal_days // year_count
    count_all = float(year_count * WIN)
    flag_row = land_mask.astype(jnp.bfloat16)[None, :]
    stacked = jnp.concatenate([daily_temps[0], flag_row], axis=0)
    extended = extended_2(stacked, (("region", 1),), 1)
    smoothed = smooth_field(
        extended[:days_in].astype(jnp.float32), extended[days_in].astype(jnp.float32)
    )
    every_year = gather_years(smoothed, "year").astype(jnp.float32)
    first_day = lax.axis_index("year") * cal_own
    coarse_rows = []
    refined_rows = []
    for j in range(cal_own):
        window = lax.dynamic_slice_in_dim(every_year, first_day + j, WIN, axis=1)
        samples = window.reshape(-1, window.shape[-1])
        coarse = coarse_from_samples(samples, count_all, BINS)
        cdf = jnp.sum(jax.nn.sigmoid((coarse[None] - samples) / KERNEL_SCALE), axis=0)
        refined = coarse - STEP_SIZE * (cdf / count_all - QUANT_LEVEL)
        coarse_rows.append(coarse)
        refined_rows.append(refined)
    return (jnp.stack(coarse_rows, axis=0), jnp.stack(refined_rows, axis=0))


def solution(mesh):
    return jax.shard_map(
        shards,
        mesh=mesh,
        in_specs=(P("year", None, "region"), P("region")),
        out_specs=(P("year", "region"), P("year", "region")),
        check_vma=False,
    )
```

```python
import jax
import jax.numpy as jnp
from jax import lax
from jax.sharding import PartitionSpec as P

WIN = 15
BINS = 256


VALUE_RANGE = 12.8
QUANT_LEVEL = 0.9
SHARPNESS = 32.0
KERNEL_SCALE = 0.25
STEP_SIZE = 2.0


def smooth_field(extended, flags):
    center = extended[..., 1:-1]
    same_west = 1.0 - jnp.abs(flags[1:-1] - flags[:-2])
    same_east = 1.0 - jnp.abs(flags[1:-1] - flags[2:])
    mixed = center + same_west * extended[..., :-2] + same_east * extended[..., 2:]
    return (mixed / (1.0 + same_west + same_east)).astype(jnp.bfloat16)


def gather_everything(block):
    devices = lax.axis_size("year") * lax.axis_size("region")
    tiled = jnp.broadcast_to(block[None], (devices,) + block.shape)
    return lax.all_to_all(tiled, ("year", "region"), 0, 0, tiled=True)


def coarse_from_samples(samples, count_all, bin_count):
    width = VALUE_RANGE / bin_count
    scaled = jnp.clip((samples + 0.5 * VALUE_RANGE) / width, 0.0, bin_count - 1.0)
    upper = lax.broadcasted_iota(jnp.float32, (bin_count, 1), 0) + 1.0
    cumulative = jnp.sum(jnp.clip(upper[None] - scaled[:, None, :], 0.0, 1.0), axis=0)
    ranks = jnp.clip(0.5 + SHARPNESS * (QUANT_LEVEL - cumulative / count_all), 0.0, 1.0)
    return -0.5 * VALUE_RANGE + width * jnp.sum(ranks, axis=0)


def shards(daily_temps, land_mask):
    days_in = daily_temps.shape[1]
    lon_own = daily_temps.shape[2]
    year_count = lax.axis_size("year")
    region_count = lax.axis_size("region")
    cal_days = days_in - WIN + 1
    cal_own = cal_days // year_count
    count_all = float(year_count * WIN)
    flag_row = land_mask.astype(jnp.bfloat16)[None, :]
    stacked = jnp.concatenate([daily_temps[0], flag_row], axis=0)
    everything = gather_everything(stacked).reshape(year_count, region_count, days_in + 1, lon_own)
    row = jnp.moveaxis(everything, 1, 2).reshape(year_count, days_in + 1, region_count * lon_own)
    ring = jnp.concatenate([row[..., -1:], row, row[..., :1]], axis=-1)
    extended = lax.dynamic_slice_in_dim(ring, lax.axis_index("region") * lon_own, lon_own + 2, axis=2)
    extended = extended.astype(jnp.float32)
    every_year = smooth_field(extended[:, :days_in], extended[0, days_in]).astype(jnp.float32)
    first_day = lax.axis_index("year") * cal_own
    coarse_rows = []
    refined_rows = []
    for j in range(cal_own):
        window = lax.dynamic_slice_in_dim(every_year, first_day + j, WIN, axis=1)
        samples = window.reshape(-1, window.shape[-1])
        coarse = coarse_from_samples(samples, count_all, BINS)
        cdf = jnp.sum(jax.nn.sigmoid((coarse[None] - samples) / KERNEL_SCALE), axis=0)
        refined = coarse - STEP_SIZE * (cdf / count_all - QUANT_LEVEL)
        coarse_rows.append(coarse)
        refined_rows.append(refined)
    return (jnp.stack(coarse_rows, axis=0), jnp.stack(refined_rows, axis=0))


def solution(mesh):
    return jax.shard_map(
        shards,
        mesh=mesh,
        in_specs=(P("year", None, "region"), P("region")),
        out_specs=(P("year", "region"), P("year", "region")),
        check_vma=False,
    )
```

```python
import jax
import jax.numpy as jnp
from jax import lax
from jax.sharding import PartitionSpec as P

WIN = 15
BINS = 256


VALUE_RANGE = 12.8
QUANT_LEVEL = 0.9
SHARPNESS = 32.0
KERNEL_SCALE = 0.25
STEP_SIZE = 2.0


def smooth_field(extended, flags):
    center = extended[..., 1:-1]
    same_west = 1.0 - jnp.abs(flags[1:-1] - flags[:-2])
    same_east = 1.0 - jnp.abs(flags[1:-1] - flags[2:])
    mixed = center + same_west * extended[..., :-2] + same_east * extended[..., 2:]
    return lax.reduce_precision(mixed / (1.0 + same_west + same_east), exponent_bits=8, mantissa_bits=7)


def gather_windows(temps, flags, span, cal_own):
    year_count, region_count = lax.axis_size("year"), lax.axis_size("region")
    chunk_rows = span + 1
    total = year_count * region_count * chunk_rows
    out_row = lax.broadcasted_iota(jnp.int32, (total, temps.shape[0]), 0)
    day = lax.broadcasted_iota(jnp.int32, (total, temps.shape[0]), 1)
    offset = out_row % chunk_rows
    first = (out_row // (chunk_rows * region_count)) * cal_own
    select = jnp.where((offset < span) & (day == first + offset), 1.0, 0.0).astype(temps.dtype)
    picked = jnp.dot(select, temps, preferred_element_type=jnp.float32)
    is_flag = (lax.broadcasted_iota(jnp.int32, (total, 1), 0) % chunk_rows) == span
    rows = jnp.where(is_flag, flags.astype(jnp.float32)[None, :], picked).astype(temps.dtype)
    rows = rows.reshape(year_count * region_count, chunk_rows, temps.shape[1])
    return lax.all_to_all(rows, ("year", "region"), 0, 0, tiled=True)


def coarse_from_samples(samples, count_all, bin_count):
    width = VALUE_RANGE / bin_count
    scaled = jnp.clip((samples + 0.5 * VALUE_RANGE) / width, 0.0, bin_count - 1.0)
    upper = lax.broadcasted_iota(jnp.float32, (bin_count, 1), 0) + 1.0
    cumulative = jnp.sum(jnp.clip(upper[None] - scaled[:, None, :], 0.0, 1.0), axis=0)
    ranks = jnp.clip(0.5 + SHARPNESS * (QUANT_LEVEL - cumulative / count_all), 0.0, 1.0)
    return -0.5 * VALUE_RANGE + width * jnp.sum(ranks, axis=0)


def shards(daily_temps, land_mask):
    days_in = daily_temps.shape[1]
    lon_own = daily_temps.shape[2]
    year_count = lax.axis_size("year")
    region_count = lax.axis_size("region")
    cal_days = days_in - WIN + 1
    cal_own = cal_days // year_count
    span = WIN + cal_own - 1
    count_all = float(year_count * WIN)
    received = gather_windows(daily_temps[0], land_mask, span, cal_own)
    received = received.reshape(year_count, region_count, span + 1, lon_own)
    row = jnp.moveaxis(received, 1, 2).reshape(year_count, span + 1, region_count * lon_own)
    ring = jnp.concatenate([row[..., -1:], row, row[..., :1]], axis=-1)
    extended = lax.dynamic_slice_in_dim(ring, lax.axis_index("region") * lon_own, lon_own + 2, axis=2)
    extended = extended.astype(jnp.float32)
    every_year = smooth_field(extended[:, :span], extended[0, span])
    coarse_rows = []
    refined_rows = []
    for j in range(cal_own):
        samples = every_year[:, j : j + WIN].reshape(-1, lon_own)
        coarse = coarse_from_samples(samples, count_all, BINS)
        cdf = jnp.sum(jax.nn.sigmoid((coarse[None] - samples) / KERNEL_SCALE), axis=0)
        refined = coarse - STEP_SIZE * (cdf / count_all - QUANT_LEVEL)
        coarse_rows.append(coarse)
        refined_rows.append(refined)
    return (jnp.stack(coarse_rows, axis=0), jnp.stack(refined_rows, axis=0))


def solution(mesh):
    return jax.shard_map(
        shards,
        mesh=mesh,
        in_specs=(P("year", None, "region"), P("region")),
        out_specs=(P("year", "region"), P("year", "region")),
        check_vma=False,
    )
```

```python
import jax
import jax.numpy as jnp
from jax import lax
from jax.sharding import PartitionSpec as P

WIN = 15
BINS = 256


VALUE_RANGE = 12.8
QUANT_LEVEL = 0.9
SHARPNESS = 32.0
KERNEL_SCALE = 0.25
STEP_SIZE = 2.0


def smooth_field(extended, flags):
    center = extended[..., 1:-1]
    same_west = 1.0 - jnp.abs(flags[1:-1] - flags[:-2])
    same_east = 1.0 - jnp.abs(flags[1:-1] - flags[2:])
    mixed = center + same_west * extended[..., :-2] + same_east * extended[..., 2:]
    return lax.reduce_precision(mixed / (1.0 + same_west + same_east), exponent_bits=8, mantissa_bits=7)


def gather_windows(temps, flags, span, cal_own):
    year_count, region_count = lax.axis_size("year"), lax.axis_size("region")
    chunk_rows = span + 1
    shape = (year_count, region_count, chunk_rows, temps.shape[0] + 1)
    year = lax.broadcasted_iota(jnp.int32, shape, 0)
    offset = lax.broadcasted_iota(jnp.int32, shape, 2)
    day = lax.broadcasted_iota(jnp.int32, shape, 3)
    wanted = jnp.where(offset < span, year * cal_own + offset, temps.shape[0])
    select = jnp.where(day == wanted, 1.0, 0.0).astype(temps.dtype)
    select = select.reshape(year_count * region_count * chunk_rows, temps.shape[0] + 1)
    source = jnp.concatenate([temps, flags.astype(temps.dtype)[None, :]], axis=0)
    rows = jnp.dot(select, source, preferred_element_type=jnp.float32).astype(temps.dtype)
    rows = rows.reshape(year_count * region_count, chunk_rows, temps.shape[1])
    return lax.all_to_all(rows, ("year", "region"), 0, 0, tiled=True)


def coarse_from_samples(samples, count_all, bin_count):
    width = VALUE_RANGE / bin_count
    scaled = jnp.clip((samples + 0.5 * VALUE_RANGE) / width, 0.0, bin_count - 1.0)
    upper = lax.broadcasted_iota(jnp.float32, (bin_count, 1), 0) + 1.0
    cumulative = jnp.sum(jnp.clip(upper[None] - scaled[:, None, :], 0.0, 1.0), axis=0)
    ranks = jnp.clip(0.5 + SHARPNESS * (QUANT_LEVEL - cumulative / count_all), 0.0, 1.0)
    return -0.5 * VALUE_RANGE + width * jnp.sum(ranks, axis=0)


def shards(daily_temps, land_mask):
    days_in = daily_temps.shape[1]
    lon_own = daily_temps.shape[2]
    year_count = lax.axis_size("year")
    region_count = lax.axis_size("region")
    cal_days = days_in - WIN + 1
    cal_own = cal_days // year_count
    span = WIN + cal_own - 1
    count_all = float(year_count * WIN)
    received = gather_windows(daily_temps[0], land_mask, span, cal_own)
    received = received.reshape(year_count, region_count, span + 1, lon_own)
    row = jnp.moveaxis(received, 1, 2).reshape(year_count, span + 1, region_count * lon_own)
    ring = jnp.concatenate([row[..., -1:], row, row[..., :1]], axis=-1)
    extended = lax.dynamic_slice_in_dim(ring, lax.axis_index("region") * lon_own, lon_own + 2, axis=2)
    extended = extended.astype(jnp.float32)
    every_year = smooth_field(extended[:, :span], extended[0, span])
    coarse_rows = []
    refined_rows = []
    for j in range(cal_own):
        samples = every_year[:, j : j + WIN].reshape(-1, lon_own)
        coarse = coarse_from_samples(samples, count_all, BINS)
        cdf = jnp.sum(jax.nn.sigmoid((coarse[None] - samples) / KERNEL_SCALE), axis=0)
        refined = coarse - STEP_SIZE * (cdf / count_all - QUANT_LEVEL)
        coarse_rows.append(coarse)
        refined_rows.append(refined)
    return (jnp.stack(coarse_rows, axis=0), jnp.stack(refined_rows, axis=0))


def solution(mesh):
    return jax.shard_map(
        shards,
        mesh=mesh,
        in_specs=(P("year", None, "region"), P("region")),
        out_specs=(P("year", "region"), P("year", "region")),
        check_vma=False,
    )
```

```python
import functools

import jax
import jax.numpy as jnp
from jax import lax
from jax.experimental import pallas as pl
from jax.experimental.pallas import tpu as pltpu
from jax.sharding import PartitionSpec as P

WIN = 15
BINS = 256


VALUE_RANGE = 12.8
QUANT_LEVEL = 0.9
SHARPNESS = 32.0
KERNEL_SCALE = 0.25
STEP_SIZE = 2.0


def smooth_field(extended, flags):
    center = extended[..., 1:-1]
    same_west = 1.0 - jnp.abs(flags[1:-1] - flags[:-2])
    same_east = 1.0 - jnp.abs(flags[1:-1] - flags[2:])
    mixed = center + same_west * extended[..., :-2] + same_east * extended[..., 2:]
    return lax.reduce_precision(mixed / (1.0 + same_west + same_east), exponent_bits=8, mantissa_bits=7)


def chunk_kernel(span, cal_own, year_count, region_count, temps_ref, mask_ref, out_ref, stage_ref):
    days_in = temps_ref.shape[0]
    chunk_rows = span + 1
    stage_ref[0:days_in, :] = temps_ref[...].astype(jnp.float32)
    flags = mask_ref[...].astype(jnp.float32)
    stage_ref[days_in : days_in + 1, :] = flags
    is_flag = lax.broadcasted_iota(jnp.int32, (chunk_rows, out_ref.shape[1]), 0) == span
    for year in range(year_count):
        rows = stage_ref[year * cal_own : year * cal_own + chunk_rows, :]
        tile = jnp.where(is_flag, flags, rows).astype(out_ref.dtype)
        for region in range(region_count):
            first = (year * region_count + region) * chunk_rows
            out_ref[first : first + chunk_rows, :] = tile


def gather_windows(temps, flags, span, cal_own):
    year_count, region_count = lax.axis_size("year"), lax.axis_size("region")
    chunk_rows = span + 1
    lon_own = temps.shape[1]
    rows = pl.pallas_call(
        functools.partial(chunk_kernel, span, cal_own, year_count, region_count),
        out_shape=jax.ShapeDtypeStruct((year_count * region_count * chunk_rows, lon_own), temps.dtype),
        scratch_shapes=[pltpu.VMEM((temps.shape[0] + 1, lon_own), jnp.float32)],
    )(temps, flags.reshape(1, lon_own))
    rows = rows.reshape(year_count * region_count, chunk_rows, lon_own)
    return lax.all_to_all(rows, ("year", "region"), 0, 0, tiled=True)


def coarse_from_samples(samples, count_all, bin_count):
    width = VALUE_RANGE / bin_count
    scaled = jnp.clip((samples + 0.5 * VALUE_RANGE) / width, 0.0, bin_count - 1.0)
    upper = lax.broadcasted_iota(jnp.float32, (bin_count, 1), 0) + 1.0
    cumulative = jnp.sum(jnp.clip(upper[None] - scaled[:, None, :], 0.0, 1.0), axis=0)
    ranks = jnp.clip(0.5 + SHARPNESS * (QUANT_LEVEL - cumulative / count_all), 0.0, 1.0)
    return -0.5 * VALUE_RANGE + width * jnp.sum(ranks, axis=0)


def shards(daily_temps, land_mask):
    days_in = daily_temps.shape[1]
    lon_own = daily_temps.shape[2]
    year_count = lax.axis_size("year")
    region_count = lax.axis_size("region")
    cal_days = days_in - WIN + 1
    cal_own = cal_days // year_count
    span = WIN + cal_own - 1
    count_all = float(year_count * WIN)
    received = gather_windows(daily_temps[0], land_mask, span, cal_own)
    received = received.reshape(year_count, region_count, span + 1, lon_own)
    row = jnp.moveaxis(received, 1, 2).reshape(year_count, span + 1, region_count * lon_own)
    ring = jnp.concatenate([row[..., -1:], row, row[..., :1]], axis=-1)
    extended = lax.dynamic_slice_in_dim(ring, lax.axis_index("region") * lon_own, lon_own + 2, axis=2)
    extended = extended.astype(jnp.float32)
    every_year = smooth_field(extended[:, :span], extended[0, span])
    coarse_rows = []
    refined_rows = []
    for j in range(cal_own):
        samples = every_year[:, j : j + WIN].reshape(-1, lon_own)
        coarse = coarse_from_samples(samples, count_all, BINS)
        cdf = jnp.sum(jax.nn.sigmoid((coarse[None] - samples) / KERNEL_SCALE), axis=0)
        refined = coarse - STEP_SIZE * (cdf / count_all - QUANT_LEVEL)
        coarse_rows.append(coarse)
        refined_rows.append(refined)
    return (jnp.stack(coarse_rows, axis=0), jnp.stack(refined_rows, axis=0))


def solution(mesh):
    return jax.shard_map(
        shards,
        mesh=mesh,
        in_specs=(P("year", None, "region"), P("region")),
        out_specs=(P("year", "region"), P("year", "region")),
        check_vma=False,
    )
```

```python
import functools

import jax
import jax.numpy as jnp
from jax import lax
from jax.experimental import pallas as pl
from jax.experimental.pallas import tpu as pltpu
from jax.sharding import PartitionSpec as P

WIN = 15
BINS = 256


VALUE_RANGE = 12.8
QUANT_LEVEL = 0.9
SHARPNESS = 32.0
KERNEL_SCALE = 0.25
STEP_SIZE = 2.0


def chunk_kernel(span, cal_own, year_count, region_count, temps_ref, mask_ref, out_ref, stage_ref):
    days_in = temps_ref.shape[0]
    chunk_rows = span + 1
    stage_ref[0:days_in, :] = temps_ref[...].astype(jnp.float32)
    flags = mask_ref[...].astype(jnp.float32)
    stage_ref[days_in : days_in + 1, :] = flags
    is_flag = lax.broadcasted_iota(jnp.int32, (chunk_rows, out_ref.shape[1]), 0) == span
    for year in range(year_count):
        rows = stage_ref[year * cal_own : year * cal_own + chunk_rows, :]
        tile = jnp.where(is_flag, flags, rows).astype(out_ref.dtype)
        for region in range(region_count):
            first = (year * region_count + region) * chunk_rows
            out_ref[first : first + chunk_rows, :] = tile


def gather_windows(temps, flags, span, cal_own):
    year_count, region_count = lax.axis_size("year"), lax.axis_size("region")
    chunk_rows = span + 1
    lon_own = temps.shape[1]
    rows = pl.pallas_call(
        functools.partial(chunk_kernel, span, cal_own, year_count, region_count),
        out_shape=jax.ShapeDtypeStruct((year_count * region_count * chunk_rows, lon_own), temps.dtype),
        scratch_shapes=[pltpu.VMEM((temps.shape[0] + 1, lon_own), jnp.float32)],
    )(temps, flags.reshape(1, lon_own))
    rows = rows.reshape(year_count * region_count, chunk_rows, lon_own)
    return lax.all_to_all(rows, ("year", "region"), 0, 0, tiled=True)


def threshold_kernel(span, cal_own, year_count, region_count, count_all, region_ref, recv_ref, coarse_ref,
                     refined_ref, samples_ref, scaled_ref):
    chunk_rows = span + 1
    lon_own = recv_ref.shape[1]
    width = VALUE_RANGE / BINS
    region = region_ref[0]
    west_region = (region + region_count - 1) % region_count
    east_region = (region + 1) % region_count
    lane = lax.broadcasted_iota(jnp.int32, (chunk_rows, lon_own), 1)

    def block(year, source):
        first = pl.multiple_of((year * region_count + source) * chunk_rows, chunk_rows)
        return recv_ref[pl.ds(first, chunk_rows), :].astype(jnp.float32)

    def neighbours(year):
        center, west, east = block(year, region), block(year, west_region), block(year, east_region)
        to_west = jnp.where(lane == 0, pltpu.roll(west, 1, 1), pltpu.roll(center, 1, 1))
        to_east = jnp.where(lane == lon_own - 1, pltpu.roll(east, lon_own - 1, 1), pltpu.roll(center, lon_own - 1, 1))
        return center, to_west, to_east

    center, to_west, to_east = neighbours(0)
    flag, flag_west, flag_east = center[span:, :], to_west[span:, :], to_east[span:, :]
    same_west = 1.0 - jnp.abs(flag - flag_west)
    same_east = 1.0 - jnp.abs(flag - flag_east)
    norm = 1.0 + same_west + same_east
    for year in range(year_count):
        center, to_west, to_east = neighbours(year)
        mixed = center + same_west * to_west + same_east * to_east
        smooth = (mixed / norm).astype(jnp.bfloat16).astype(jnp.float32)
        samples_ref[year * chunk_rows : (year + 1) * chunk_rows, :] = smooth
    samples_total = year_count * WIN
    upper = lax.broadcasted_iota(jnp.int32, (64, lon_own), 0).astype(jnp.float32) + 1.0
    for j in range(cal_own):
        for year in range(year_count):
            rows = samples_ref[year * chunk_rows + j : year * chunk_rows + j + WIN, :]
            scaled = jnp.clip((rows + 0.5 * VALUE_RANGE) / width, 0.0, BINS - 1.0)
            scaled_ref[year * WIN : (year + 1) * WIN, :] = scaled
        total = jnp.zeros((1, lon_own), jnp.float32)
        for part in range(BINS // 64):
            def add_sample(index, cumulative):
                row = scaled_ref[pl.ds(index, 1), :]
                return cumulative + jnp.clip(upper + float(64 * part) - row, 0.0, 1.0)

            cumulative = lax.fori_loop(0, samples_total, add_sample, jnp.zeros((64, lon_own), jnp.float32))
            ranks = jnp.clip(0.5 + SHARPNESS * (QUANT_LEVEL - cumulative / count_all), 0.0, 1.0)
            total = total + jnp.sum(ranks, axis=0, keepdims=True)
        coarse = -0.5 * VALUE_RANGE + width * total
        cdf = jnp.zeros((1, lon_own), jnp.float32)
        for year in range(year_count):
            rows = samples_ref[year * chunk_rows + j : year * chunk_rows + j + WIN, :]
            kernel = 1.0 / (1.0 + jnp.exp(-((coarse - rows) / KERNEL_SCALE)))
            cdf = cdf + jnp.sum(kernel, axis=0, keepdims=True)
        coarse_ref[j : j + 1, :] = coarse
        refined_ref[j : j + 1, :] = coarse - STEP_SIZE * (cdf / count_all - QUANT_LEVEL)


def shards(daily_temps, land_mask):
    days_in = daily_temps.shape[1]
    lon_own = daily_temps.shape[2]
    year_count = lax.axis_size("year")
    region_count = lax.axis_size("region")
    cal_days = days_in - WIN + 1
    cal_own = cal_days // year_count
    span = WIN + cal_own - 1
    count_all = float(year_count * WIN)
    received = gather_windows(daily_temps[0], land_mask, span, cal_own)
    received = received.reshape(year_count * region_count * (span + 1), lon_own)
    region = lax.axis_index("region").astype(jnp.int32).reshape(1)
    out = jax.ShapeDtypeStruct((cal_own, lon_own), jnp.float32)
    return pl.pallas_call(
        functools.partial(threshold_kernel, span, cal_own, year_count, region_count, count_all),
        out_shape=(out, out),
        in_specs=[pl.BlockSpec(memory_space=pltpu.SMEM), pl.BlockSpec(memory_space=pltpu.VMEM)],
        scratch_shapes=[
            pltpu.VMEM((year_count * (span + 1), lon_own), jnp.float32),
            pltpu.VMEM((year_count * WIN, lon_own), jnp.float32),
        ],
    )(region, received)


def solution(mesh):
    return jax.shard_map(
        shards,
        mesh=mesh,
        in_specs=(P("year", None, "region"), P("region")),
        out_specs=(P("year", "region"), P("year", "region")),
        check_vma=False,
    )
```

```python
import functools

import jax
import jax.numpy as jnp
from jax import lax
from jax.experimental import pallas as pl
from jax.experimental.pallas import tpu as pltpu
from jax.sharding import PartitionSpec as P

WIN = 15
BINS = 256


VALUE_RANGE = 12.8
QUANT_LEVEL = 0.9
SHARPNESS = 32.0
KERNEL_SCALE = 0.25
STEP_SIZE = 2.0


def smooth_field(extended, flags):
    center = extended[..., 1:-1]
    same_west = 1.0 - jnp.abs(flags[1:-1] - flags[:-2])
    same_east = 1.0 - jnp.abs(flags[1:-1] - flags[2:])
    mixed = center + same_west * extended[..., :-2] + same_east * extended[..., 2:]
    return lax.reduce_precision(mixed / (1.0 + same_west + same_east), exponent_bits=8, mantissa_bits=7)


def chunk_kernel(span, cal_own, year_count, region_count, temps_ref, mask_ref, out_ref, stage_ref):
    days_in = temps_ref.shape[0]
    chunk_rows = span + 1
    stage_ref[0:days_in, :] = temps_ref[...].astype(jnp.float32)
    flags = mask_ref[...].astype(jnp.float32)
    stage_ref[days_in : days_in + 1, :] = flags
    is_flag = lax.broadcasted_iota(jnp.int32, (chunk_rows, out_ref.shape[1]), 0) == span
    for year in range(year_count):
        rows = stage_ref[year * cal_own : year * cal_own + chunk_rows, :]
        tile = jnp.where(is_flag, flags, rows).astype(out_ref.dtype)
        for region in range(region_count):
            first = (year * region_count + region) * chunk_rows
            out_ref[first : first + chunk_rows, :] = tile


def gather_windows(temps, flags, span, cal_own):
    year_count, region_count = lax.axis_size("year"), lax.axis_size("region")
    chunk_rows = span + 1
    lon_own = temps.shape[1]
    rows = pl.pallas_call(
        functools.partial(chunk_kernel, span, cal_own, year_count, region_count),
        out_shape=jax.ShapeDtypeStruct((year_count * region_count * chunk_rows, lon_own), temps.dtype),
        scratch_shapes=[pltpu.VMEM((temps.shape[0] + 1, lon_own), jnp.float32)],
    )(temps, flags.reshape(1, lon_own))
    rows = rows.reshape(year_count * region_count, chunk_rows, lon_own)
    return lax.all_to_all(rows, ("year", "region"), 0, 0, tiled=True)


def coarse_from_samples(samples, count_all, bin_count):
    width = VALUE_RANGE / bin_count
    scaled = jnp.clip((samples + 0.5 * VALUE_RANGE) / width, 0.0, bin_count - 1.0)
    grouped = scaled.reshape(-1, WIN, scaled.shape[-1])
    points = lax.broadcasted_iota(jnp.float32, (bin_count + 8, 1), 0)
    partial = jnp.sum(jnp.minimum(grouped[:, :, None, :], points[None, None]), axis=1)
    floor_sum = jnp.sum(partial, axis=0)
    cumulative = count_all - (floor_sum[1 : bin_count + 1] - floor_sum[:bin_count])
    ranks = jnp.clip(0.5 + SHARPNESS * (QUANT_LEVEL - cumulative / count_all), 0.0, 1.0)
    return -0.5 * VALUE_RANGE + width * jnp.sum(ranks, axis=0)


def shards(daily_temps, land_mask):
    days_in = daily_temps.shape[1]
    lon_own = daily_temps.shape[2]
    year_count = lax.axis_size("year")
    region_count = lax.axis_size("region")
    cal_days = days_in - WIN + 1
    cal_own = cal_days // year_count
    span = WIN + cal_own - 1
    count_all = float(year_count * WIN)
    received = gather_windows(daily_temps[0], land_mask, span, cal_own)
    received = received.reshape(year_count, region_count, span + 1, lon_own)
    row = jnp.moveaxis(received, 1, 2).reshape(year_count, span + 1, region_count * lon_own)
    ring = jnp.concatenate([row[..., -1:], row, row[..., :1]], axis=-1)
    extended = lax.dynamic_slice_in_dim(ring, lax.axis_index("region") * lon_own, lon_own + 2, axis=2)
    extended = extended.astype(jnp.float32)
    every_year = smooth_field(extended[:, :span], extended[0, span])
    coarse_rows = []
    refined_rows = []
    for j in range(cal_own):
        samples = every_year[:, j : j + WIN].reshape(-1, lon_own)
        coarse = coarse_from_samples(samples, count_all, BINS)
        cdf = jnp.sum(jax.nn.sigmoid((coarse[None] - samples) / KERNEL_SCALE), axis=0)
        refined = coarse - STEP_SIZE * (cdf / count_all - QUANT_LEVEL)
        coarse_rows.append(coarse)
        refined_rows.append(refined)
    return (jnp.stack(coarse_rows, axis=0), jnp.stack(refined_rows, axis=0))


def solution(mesh):
    return jax.shard_map(
        shards,
        mesh=mesh,
        in_specs=(P("year", None, "region"), P("region")),
        out_specs=(P("year", "region"), P("year", "region")),
        check_vma=False,
    )
```

```python
import functools

import jax
import jax.numpy as jnp
from jax import lax
from jax.experimental import pallas as pl
from jax.experimental.pallas import tpu as pltpu
from jax.sharding import PartitionSpec as P

WIN = 15
BINS = 256


VALUE_RANGE = 12.8
QUANT_LEVEL = 0.9
SHARPNESS = 32.0
KERNEL_SCALE = 0.25
STEP_SIZE = 2.0


def smooth_field(extended, flags):
    center = extended[..., 1:-1]
    same_west = 1.0 - jnp.abs(flags[1:-1] - flags[:-2])
    same_east = 1.0 - jnp.abs(flags[1:-1] - flags[2:])
    mixed = center + same_west * extended[..., :-2] + same_east * extended[..., 2:]
    return lax.reduce_precision(mixed / (1.0 + same_west + same_east), exponent_bits=8, mantissa_bits=7)


def chunk_kernel(span, cal_own, year_count, region_count, temps_ref, mask_ref, out_ref, stage_ref):
    days_in = temps_ref.shape[0]
    chunk_rows = span + 1
    stage_ref[0:days_in, :] = temps_ref[...].astype(jnp.float32)
    flags = mask_ref[...].astype(jnp.float32)
    stage_ref[days_in : days_in + 1, :] = flags
    is_flag = lax.broadcasted_iota(jnp.int32, (chunk_rows, out_ref.shape[1]), 0) == span
    for year in range(year_count):
        rows = stage_ref[year * cal_own : year * cal_own + chunk_rows, :]
        tile = jnp.where(is_flag, flags, rows).astype(out_ref.dtype)
        for region in range(region_count):
            first = (region * year_count + year) * chunk_rows
            out_ref[first : first + chunk_rows, :] = tile


def gather_windows(temps, flags, span, cal_own):
    year_count, region_count = lax.axis_size("year"), lax.axis_size("region")
    chunk_rows = span + 1
    lon_own = temps.shape[1]
    rows = pl.pallas_call(
        functools.partial(chunk_kernel, span, cal_own, year_count, region_count),
        out_shape=jax.ShapeDtypeStruct((year_count * region_count * chunk_rows, lon_own), temps.dtype),
        scratch_shapes=[pltpu.VMEM((temps.shape[0] + 1, lon_own), jnp.float32)],
    )(temps, flags.reshape(1, lon_own))
    rows = rows.reshape(year_count * region_count, chunk_rows, lon_own)
    return lax.all_to_all(rows, ("region", "year"), 0, 0, tiled=True)


def coarse_from_samples(samples, count_all, bin_count):
    width = VALUE_RANGE / bin_count
    scaled = jnp.clip((samples + 0.5 * VALUE_RANGE) / width, 0.0, bin_count - 1.0)
    grouped = scaled.reshape(-1, WIN, scaled.shape[-1])
    points = lax.broadcasted_iota(jnp.float32, (bin_count + 8, 1), 0)
    partial = jnp.sum(jnp.minimum(grouped[:, :, None, :], points[None, None]), axis=1)
    floor_sum = jnp.sum(partial, axis=0)
    cumulative = count_all - (floor_sum[1 : bin_count + 1] - floor_sum[:bin_count])
    ranks = jnp.clip(0.5 + SHARPNESS * (QUANT_LEVEL - cumulative / count_all), 0.0, 1.0)
    return -0.5 * VALUE_RANGE + width * jnp.sum(ranks, axis=0)


def shards(daily_temps, land_mask):
    days_in = daily_temps.shape[1]
    lon_own = daily_temps.shape[2]
    year_count = lax.axis_size("year")
    region_count = lax.axis_size("region")
    cal_days = days_in - WIN + 1
    cal_own = cal_days // year_count
    span = WIN + cal_own - 1
    count_all = float(year_count * WIN)
    received = gather_windows(daily_temps[0], land_mask, span, cal_own)
    received = received.reshape(region_count, year_count, span + 1, lon_own)
    row = jnp.transpose(received, (1, 2, 0, 3)).reshape(year_count, span + 1, region_count * lon_own)
    ring = jnp.concatenate([row[..., -1:], row, row[..., :1]], axis=-1)
    extended = lax.dynamic_slice_in_dim(ring, lax.axis_index("region") * lon_own, lon_own + 2, axis=2)
    extended = extended.astype(jnp.float32)
    every_year = smooth_field(extended[:, :span], extended[0, span])
    coarse_rows = []
    refined_rows = []
    for j in range(cal_own):
        samples = every_year[:, j : j + WIN].reshape(-1, lon_own)
        coarse = coarse_from_samples(samples, count_all, BINS)
        cdf = jnp.sum(jax.nn.sigmoid((coarse[None] - samples) / KERNEL_SCALE), axis=0)
        refined = coarse - STEP_SIZE * (cdf / count_all - QUANT_LEVEL)
        coarse_rows.append(coarse)
        refined_rows.append(refined)
    return (jnp.stack(coarse_rows, axis=0), jnp.stack(refined_rows, axis=0))


def solution(mesh):
    return jax.shard_map(
        shards,
        mesh=mesh,
        in_specs=(P("year", None, "region"), P("region")),
        out_specs=(P("year", "region"), P("year", "region")),
        check_vma=False,
    )
```

```python
import functools

import jax
import jax.numpy as jnp
from jax import lax
from jax.experimental import pallas as pl
from jax.experimental.pallas import tpu as pltpu
from jax.sharding import PartitionSpec as P

WIN = 15
BINS = 256


VALUE_RANGE = 12.8
QUANT_LEVEL = 0.9
SHARPNESS = 32.0
KERNEL_SCALE = 0.25
STEP_SIZE = 2.0


def smooth_field(extended, flags):
    center = extended[..., 1:-1]
    same_west = 1.0 - jnp.abs(flags[1:-1] - flags[:-2])
    same_east = 1.0 - jnp.abs(flags[1:-1] - flags[2:])
    mixed = center + same_west * extended[..., :-2] + same_east * extended[..., 2:]
    return lax.reduce_precision(mixed / (1.0 + same_west + same_east), exponent_bits=8, mantissa_bits=7)


def chunk_kernel(span, cal_own, year_count, region_count, temps_ref, mask_ref, out_ref, stage_ref):
    days_in = temps_ref.shape[0]
    chunk_rows = span + 1
    stage_ref[0:days_in, :] = temps_ref[...].astype(jnp.float32)
    flags = mask_ref[...].astype(jnp.float32)
    stage_ref[days_in : days_in + 1, :] = flags
    is_flag = lax.broadcasted_iota(jnp.int32, (chunk_rows, out_ref.shape[1]), 0) == span
    for year in range(year_count):
        rows = stage_ref[year * cal_own : year * cal_own + chunk_rows, :]
        tile = jnp.where(is_flag, flags, rows).astype(out_ref.dtype)
        for region in range(region_count):
            first = (region * year_count + year) * chunk_rows
            out_ref[first : first + chunk_rows, :] = tile


def gather_windows(temps, flags, span, cal_own):
    year_count, region_count = lax.axis_size("year"), lax.axis_size("region")
    chunk_rows = span + 1
    lon_own = temps.shape[1]
    rows = pl.pallas_call(
        functools.partial(chunk_kernel, span, cal_own, year_count, region_count),
        out_shape=jax.ShapeDtypeStruct((year_count * region_count * chunk_rows, lon_own), temps.dtype),
        scratch_shapes=[pltpu.VMEM((temps.shape[0] + 1, lon_own), jnp.float32)],
    )(temps, flags.reshape(1, lon_own))
    rows = rows.reshape(year_count * region_count, chunk_rows, lon_own)
    return lax.all_to_all(rows, ("region", "year"), 0, 0, tiled=True)


def coarse_from_samples(samples, count_all, bin_count):
    width = VALUE_RANGE / bin_count
    scaled = jnp.clip((samples + 0.5 * VALUE_RANGE) / width, 0.0, bin_count - 1.0)
    grouped = scaled.reshape(-1, WIN, scaled.shape[-1])
    points = lax.broadcasted_iota(jnp.float32, (bin_count + 8, 1), 0)
    partial = jnp.sum(jnp.minimum(grouped[:, :, None, :], points[None, None]), axis=1)
    floor_sum = jnp.sum(partial, axis=0)
    cumulative = count_all - (floor_sum[1 : bin_count + 1] - floor_sum[:bin_count])
    ranks = jnp.clip(0.5 + SHARPNESS * (QUANT_LEVEL - cumulative / count_all), 0.0, 1.0)
    return -0.5 * VALUE_RANGE + width * jnp.sum(ranks, axis=0)


def shards(daily_temps, land_mask):
    days_in = daily_temps.shape[1]
    lon_own = daily_temps.shape[2]
    year_count = lax.axis_size("year")
    region_count = lax.axis_size("region")
    cal_days = days_in - WIN + 1
    cal_own = cal_days // year_count
    span = WIN + cal_own - 1
    count_all = float(year_count * WIN)
    received = gather_windows(daily_temps[0], land_mask, span, cal_own)
    received = received.reshape(region_count, year_count, span + 1, lon_own)
    region = lax.axis_index("region")
    center = lax.dynamic_index_in_dim(received, region, 0, keepdims=False)
    west = lax.dynamic_index_in_dim(received, lax.rem(region + region_count - 1, region_count), 0, keepdims=False)
    east = lax.dynamic_index_in_dim(received, lax.rem(region + 1, region_count), 0, keepdims=False)
    extended = jnp.concatenate([west[..., -1:], center, east[..., :1]], axis=-1)
    extended = extended.astype(jnp.float32)
    every_year = smooth_field(extended[:, :span], extended[0, span])
    coarse_rows = []
    refined_rows = []
    for j in range(cal_own):
        samples = every_year[:, j : j + WIN].reshape(-1, lon_own)
        coarse = coarse_from_samples(samples, count_all, BINS)
        cdf = jnp.sum(jax.nn.sigmoid((coarse[None] - samples) / KERNEL_SCALE), axis=0)
        refined = coarse - STEP_SIZE * (cdf / count_all - QUANT_LEVEL)
        coarse_rows.append(coarse)
        refined_rows.append(refined)
    return (jnp.stack(coarse_rows, axis=0), jnp.stack(refined_rows, axis=0))


def solution(mesh):
    return jax.shard_map(
        shards,
        mesh=mesh,
        in_specs=(P("year", None, "region"), P("region")),
        out_specs=(P("year", "region"), P("year", "region")),
        check_vma=False,
    )
```

```python
import functools

import jax
import jax.numpy as jnp
from jax import lax
from jax.experimental import pallas as pl
from jax.experimental.pallas import tpu as pltpu
from jax.sharding import PartitionSpec as P

WIN = 15
BINS = 256


VALUE_RANGE = 12.8
QUANT_LEVEL = 0.9
SHARPNESS = 32.0
KERNEL_SCALE = 0.25
STEP_SIZE = 2.0


def smooth_field(extended, flags):
    center = extended[..., 1:-1]
    same_west = 1.0 - jnp.abs(flags[1:-1] - flags[:-2])
    same_east = 1.0 - jnp.abs(flags[1:-1] - flags[2:])
    mixed = center + same_west * extended[..., :-2] + same_east * extended[..., 2:]
    return lax.reduce_precision(mixed / (1.0 + same_west + same_east), exponent_bits=8, mantissa_bits=7)


def gather_blocks(temps, flags):
    year_count, region_count = lax.axis_size("year"), lax.axis_size("region")
    days_in, lon_own = temps.shape
    row = lax.broadcasted_iota(jnp.int32, (days_in + 1, lon_own), 0)
    block = jnp.where(row == days_in, flags.astype(temps.dtype)[None, :], jnp.pad(temps, ((0, 1), (0, 0))))
    tiled = jnp.broadcast_to(block[None], (region_count * year_count, days_in + 1, lon_own))
    return lax.all_to_all(tiled, ("region", "year"), 0, 0, tiled=True)


def coarse_from_samples(samples, count_all, bin_count):
    width = VALUE_RANGE / bin_count
    scaled = jnp.clip((samples + 0.5 * VALUE_RANGE) / width, 0.0, bin_count - 1.0)
    grouped = scaled.reshape(-1, WIN, scaled.shape[-1])
    points = lax.broadcasted_iota(jnp.float32, (bin_count + 8, 1), 0)
    partial = jnp.sum(jnp.minimum(grouped[:, :, None, :], points[None, None]), axis=1)
    floor_sum = jnp.sum(partial, axis=0)
    cumulative = count_all - (floor_sum[1 : bin_count + 1] - floor_sum[:bin_count])
    ranks = jnp.clip(0.5 + SHARPNESS * (QUANT_LEVEL - cumulative / count_all), 0.0, 1.0)
    return -0.5 * VALUE_RANGE + width * jnp.sum(ranks, axis=0)


def shards(daily_temps, land_mask):
    days_in = daily_temps.shape[1]
    lon_own = daily_temps.shape[2]
    year_count = lax.axis_size("year")
    region_count = lax.axis_size("region")
    cal_days = days_in - WIN + 1
    cal_own = cal_days // year_count
    span = WIN + cal_own - 1
    count_all = float(year_count * WIN)
    received = gather_blocks(daily_temps[0], land_mask)
    received = received.reshape(region_count, year_count, days_in + 1, lon_own)
    region = lax.axis_index("region")
    first_day = lax.axis_index("year") * cal_own

    def window(index):
        picked = lax.dynamic_index_in_dim(received, index, 0, keepdims=False)
        days = lax.dynamic_slice_in_dim(picked, first_day, span, axis=1)
        return jnp.concatenate([days, picked[:, days_in:]], axis=1)

    center = window(region)
    west = window(lax.rem(region + region_count - 1, region_count))
    east = window(lax.rem(region + 1, region_count))
    extended = jnp.concatenate([west[..., -1:], center, east[..., :1]], axis=-1)
    extended = extended.astype(jnp.float32)
    every_year = smooth_field(extended[:, :span], extended[0, span])
    coarse_rows = []
    refined_rows = []
    for j in range(cal_own):
        samples = every_year[:, j : j + WIN].reshape(-1, lon_own)
        coarse = coarse_from_samples(samples, count_all, BINS)
        cdf = jnp.sum(jax.nn.sigmoid((coarse[None] - samples) / KERNEL_SCALE), axis=0)
        refined = coarse - STEP_SIZE * (cdf / count_all - QUANT_LEVEL)
        coarse_rows.append(coarse)
        refined_rows.append(refined)
    return (jnp.stack(coarse_rows, axis=0), jnp.stack(refined_rows, axis=0))


def solution(mesh):
    return jax.shard_map(
        shards,
        mesh=mesh,
        in_specs=(P("year", None, "region"), P("region")),
        out_specs=(P("year", "region"), P("year", "region")),
        check_vma=False,
    )
```

```python
import functools

import jax
import jax.numpy as jnp
from jax import lax
from jax.experimental import pallas as pl
from jax.experimental.pallas import tpu as pltpu
from jax.sharding import PartitionSpec as P

WIN = 15
BINS = 256


VALUE_RANGE = 12.8
QUANT_LEVEL = 0.9
SHARPNESS = 32.0
KERNEL_SCALE = 0.25
STEP_SIZE = 2.0


def chunk_kernel(span, cal_own, year_count, region_count, temps_ref, mask_ref, out_ref, stage_ref):
    days_in = temps_ref.shape[0]
    chunk_rows = span + 1
    stage_ref[0:days_in, :] = temps_ref[...].astype(jnp.float32)
    flags = mask_ref[...].astype(jnp.float32)
    stage_ref[days_in : days_in + 1, :] = flags
    is_flag = lax.broadcasted_iota(jnp.int32, (chunk_rows, out_ref.shape[1]), 0) == span
    for year in range(year_count):
        rows = stage_ref[year * cal_own : year * cal_own + chunk_rows, :]
        tile = jnp.where(is_flag, flags, rows).astype(out_ref.dtype)
        for region in range(region_count):
            first = (region * year_count + year) * chunk_rows
            out_ref[first : first + chunk_rows, :] = tile


def gather_windows(temps, flags, span, cal_own):
    year_count, region_count = lax.axis_size("year"), lax.axis_size("region")
    chunk_rows = span + 1
    lon_own = temps.shape[1]
    rows = pl.pallas_call(
        functools.partial(chunk_kernel, span, cal_own, year_count, region_count),
        out_shape=jax.ShapeDtypeStruct((year_count * region_count * chunk_rows, lon_own), temps.dtype),
        scratch_shapes=[pltpu.VMEM((temps.shape[0] + 1, lon_own), jnp.float32)],
    )(temps, flags.reshape(1, lon_own))
    rows = rows.reshape(year_count * region_count, chunk_rows, lon_own)
    return lax.all_to_all(rows, ("region", "year"), 0, 0, tiled=True)


def coarse_from_samples(samples, count_all, bin_count):
    width = VALUE_RANGE / bin_count
    scaled = jnp.clip((samples + 0.5 * VALUE_RANGE) / width, 0.0, bin_count - 1.0)
    grouped = scaled.reshape(-1, WIN, scaled.shape[-1])
    points = lax.broadcasted_iota(jnp.float32, (bin_count + 8, 1), 0)
    partial = jnp.sum(jnp.minimum(grouped[:, :, None, :], points[None, None]), axis=1)
    floor_sum = jnp.sum(partial, axis=0)
    cumulative = count_all - (floor_sum[1 : bin_count + 1] - floor_sum[:bin_count])
    ranks = jnp.clip(0.5 + SHARPNESS * (QUANT_LEVEL - cumulative / count_all), 0.0, 1.0)
    return -0.5 * VALUE_RANGE + width * jnp.sum(ranks, axis=0)


def shards(daily_temps, land_mask):
    days_in = daily_temps.shape[1]
    lon_own = daily_temps.shape[2]
    year_count = lax.axis_size("year")
    region_count = lax.axis_size("region")
    cal_days = days_in - WIN + 1
    cal_own = cal_days // year_count
    span = WIN + cal_own - 1
    count_all = float(year_count * WIN)
    received = gather_windows(daily_temps[0], land_mask, span, cal_own)
    received = received.reshape(region_count, year_count, span + 1, lon_own)
    region = lax.axis_index("region")
    center = lax.dynamic_index_in_dim(received, region, 0, keepdims=False)
    west = lax.dynamic_index_in_dim(received, lax.rem(region + region_count - 1, region_count), 0, keepdims=False)
    east = lax.dynamic_index_in_dim(received, lax.rem(region + 1, region_count), 0, keepdims=False)
    center = center.astype(jnp.float32)
    to_west = jnp.concatenate([west[..., -1:].astype(jnp.float32), center[..., :-1]], axis=-1)
    to_east = jnp.concatenate([center[..., 1:], east[..., :1].astype(jnp.float32)], axis=-1)
    same_west = 1.0 - jnp.abs(center[0, span] - to_west[0, span])
    same_east = 1.0 - jnp.abs(center[0, span] - to_east[0, span])
    mixed = center[:, :span] + same_west * to_west[:, :span] + same_east * to_east[:, :span]
    every_year = lax.reduce_precision(mixed / (1.0 + same_west + same_east), exponent_bits=8, mantissa_bits=7)
    coarse_rows = []
    refined_rows = []
    for j in range(cal_own):
        samples = every_year[:, j : j + WIN].reshape(-1, lon_own)
        coarse = coarse_from_samples(samples, count_all, BINS)
        cdf = jnp.sum(jax.nn.sigmoid((coarse[None] - samples) / KERNEL_SCALE), axis=0)
        refined = coarse - STEP_SIZE * (cdf / count_all - QUANT_LEVEL)
        coarse_rows.append(coarse)
        refined_rows.append(refined)
    return (jnp.stack(coarse_rows, axis=0), jnp.stack(refined_rows, axis=0))


def solution(mesh):
    return jax.shard_map(
        shards,
        mesh=mesh,
        in_specs=(P("year", None, "region"), P("region")),
        out_specs=(P("year", "region"), P("year", "region")),
        check_vma=False,
    )
```

```python
import functools

import jax
import jax.numpy as jnp
from jax import lax
from jax.experimental import pallas as pl
from jax.experimental.pallas import tpu as pltpu
from jax.sharding import PartitionSpec as P

WIN = 15
BINS = 256


VALUE_RANGE = 12.8
QUANT_LEVEL = 0.9
SHARPNESS = 32.0
KERNEL_SCALE = 0.25
STEP_SIZE = 2.0


def chunk_kernel(span, cal_own, year_count, region_count, temps_ref, mask_ref, out_ref, stage_ref):
    days_in = temps_ref.shape[0]
    chunk_rows = span + 1
    stage_ref[0:days_in, :] = temps_ref[...].astype(jnp.float32)
    flags = mask_ref[...].astype(jnp.float32)
    stage_ref[days_in : days_in + 1, :] = flags
    is_flag = lax.broadcasted_iota(jnp.int32, (chunk_rows, out_ref.shape[1]), 0) == span
    for year in range(year_count):
        rows = stage_ref[year * cal_own : year * cal_own + chunk_rows, :]
        tile = jnp.where(is_flag, flags, rows).astype(out_ref.dtype)
        for region in range(region_count):
            first = (region * year_count + year) * chunk_rows
            out_ref[first : first + chunk_rows, :] = tile


def gather_windows(temps, flags, span, cal_own):
    year_count, region_count = lax.axis_size("year"), lax.axis_size("region")
    chunk_rows = span + 1
    lon_own = temps.shape[1]
    rows = pl.pallas_call(
        functools.partial(chunk_kernel, span, cal_own, year_count, region_count),
        out_shape=jax.ShapeDtypeStruct((year_count * region_count * chunk_rows, lon_own), temps.dtype),
        scratch_shapes=[pltpu.VMEM((temps.shape[0] + 1, lon_own), jnp.float32)],
    )(temps, flags.reshape(1, lon_own))
    rows = rows.reshape(year_count * region_count, chunk_rows, lon_own)
    return lax.all_to_all(rows, ("region", "year"), 0, 0, tiled=True)


def coarse_from_samples(samples, count_all, bin_count):
    width = VALUE_RANGE / bin_count
    scaled = jnp.clip((samples + 0.5 * VALUE_RANGE) / width, 0.0, bin_count - 1.0)
    grouped = scaled.reshape(-1, WIN, scaled.shape[-1])
    points = lax.broadcasted_iota(jnp.float32, (bin_count + 8, 1), 0)
    partial = jnp.sum(jnp.minimum(grouped[:, :, None, :], points[None, None]), axis=1)
    floor_sum = jnp.sum(partial, axis=0)
    cumulative = count_all - (floor_sum[1 : bin_count + 1] - floor_sum[:bin_count])
    ranks = jnp.clip(0.5 + SHARPNESS * (QUANT_LEVEL - cumulative / count_all), 0.0, 1.0)
    return -0.5 * VALUE_RANGE + width * jnp.sum(ranks, axis=0)


def threshold_kernel(span, cal_own, year_count, region_count, count_all, region_ref, recv_ref, coarse_ref,
                     refined_ref, blocks_ref, samples_ref, scaled_ref, floor_ref, sems):
    chunk_rows = span + 1
    rows_per_region = year_count * chunk_rows
    lon_own = recv_ref.shape[1]
    width = VALUE_RANGE / BINS
    region = region_ref[0]
    sources = (region, lax.rem(region + region_count - 1, region_count), lax.rem(region + 1, region_count))
    copies = []
    for slot, source in enumerate(sources):
        first = pl.multiple_of(source * rows_per_region, chunk_rows)
        copy = pltpu.make_async_copy(recv_ref.at[pl.ds(first, rows_per_region)], blocks_ref.at[slot], sems.at[slot])
        copy.start()
        copies.append(copy)
    for copy in copies:
        copy.wait()
    lane = lax.broadcasted_iota(jnp.int32, (chunk_rows, lon_own), 1)

    def neighbours(year):
        rows = slice(year * chunk_rows, (year + 1) * chunk_rows)
        center = blocks_ref[0, rows, :].astype(jnp.float32)
        west = blocks_ref[1, rows, :].astype(jnp.float32)
        east = blocks_ref[2, rows, :].astype(jnp.float32)
        to_west = jnp.where(lane == 0, pltpu.roll(west, 1, 1), pltpu.roll(center, 1, 1))
        to_east = jnp.where(lane == lon_own - 1, pltpu.roll(east, lon_own - 1, 1), pltpu.roll(center, lon_own - 1, 1))
        return center, to_west, to_east

    center, to_west, to_east = neighbours(0)
    flag = center[span:, :]
    same_west = 1.0 - jnp.abs(flag - to_west[span:, :])
    same_east = 1.0 - jnp.abs(flag - to_east[span:, :])
    norm = 1.0 + same_west + same_east
    for year in range(year_count):
        center, to_west, to_east = neighbours(year)
        mixed = center + same_west * to_west + same_east * to_east
        samples_ref[year * chunk_rows : (year + 1) * chunk_rows, :] = (mixed / norm).astype(jnp.bfloat16).astype(jnp.float32)
    samples_total = year_count * WIN
    part_rows = (BINS + 8) // 3
    for j in range(cal_own):
        for year in range(year_count):
            rows = samples_ref[year * chunk_rows + j : year * chunk_rows + j + WIN, :]
            scaled_ref[year * WIN : (year + 1) * WIN, :] = jnp.clip((rows + 0.5 * VALUE_RANGE) / width, 0.0, BINS - 1.0)
        for part in range(3):
            points = lax.broadcasted_iota(jnp.int32, (part_rows, lon_own), 0).astype(jnp.float32) + float(part * part_rows)
            total = jnp.zeros((part_rows, lon_own), jnp.float32)
            for index in range(samples_total):
                total = total + jnp.minimum(scaled_ref[index : index + 1, :], points)
            floor_ref[part * part_rows : (part + 1) * part_rows, :] = total
        cumulative = count_all - (floor_ref[1 : BINS + 1, :] - floor_ref[0:BINS, :])
        ranks = jnp.clip(0.5 + SHARPNESS * (QUANT_LEVEL - cumulative / count_all), 0.0, 1.0)
        coarse = -0.5 * VALUE_RANGE + width * jnp.sum(ranks, axis=0, keepdims=True)
        cdf = jnp.zeros((1, lon_own), jnp.float32)
        for year in range(year_count):
            rows = samples_ref[year * chunk_rows + j : year * chunk_rows + j + WIN, :]
            cdf = cdf + jnp.sum(1.0 / (1.0 + jnp.exp(-((coarse - rows) / KERNEL_SCALE))), axis=0, keepdims=True)
        coarse_ref[j : j + 1, :] = coarse
        refined_ref[j : j + 1, :] = coarse - STEP_SIZE * (cdf / count_all - QUANT_LEVEL)


def shards(daily_temps, land_mask):
    days_in = daily_temps.shape[1]
    lon_own = daily_temps.shape[2]
    year_count = lax.axis_size("year")
    region_count = lax.axis_size("region")
    cal_days = days_in - WIN + 1
    cal_own = cal_days // year_count
    span = WIN + cal_own - 1
    count_all = float(year_count * WIN)
    received = gather_windows(daily_temps[0], land_mask, span, cal_own)
    received = received.reshape(region_count * year_count * (span + 1), lon_own)
    region = lax.axis_index("region").astype(jnp.int32).reshape(1)
    out = jax.ShapeDtypeStruct((cal_own, lon_own), jnp.float32)
    return pl.pallas_call(
        functools.partial(threshold_kernel, span, cal_own, year_count, region_count, count_all),
        out_shape=(out, out),
        in_specs=[pl.BlockSpec(memory_space=pltpu.SMEM), pl.BlockSpec(memory_space=pl.ANY)],
        scratch_shapes=[
            pltpu.VMEM((3, year_count * (span + 1), lon_own), jnp.bfloat16),
            pltpu.VMEM((year_count * (span + 1), lon_own), jnp.float32),
            pltpu.VMEM((year_count * WIN, lon_own), jnp.float32),
            pltpu.VMEM(((BINS + 8) // 3 * 3, lon_own), jnp.float32),
            pltpu.SemaphoreType.DMA((3,)),
        ],
    )(region, received)


def solution(mesh):
    return jax.shard_map(
        shards,
        mesh=mesh,
        in_specs=(P("year", None, "region"), P("region")),
        out_specs=(P("year", "region"), P("year", "region")),
        check_vma=False,
    )
```

```python
import functools

import jax
import jax.numpy as jnp
from jax import lax
from jax.experimental import pallas as pl
from jax.experimental.pallas import tpu as pltpu
from jax.sharding import PartitionSpec as P

WIN = 15
BINS = 256


VALUE_RANGE = 12.8
QUANT_LEVEL = 0.9
SHARPNESS = 32.0
KERNEL_SCALE = 0.25
STEP_SIZE = 2.0


def chunk_kernel(span, cal_own, year_count, region_count, temps_ref, mask_ref, out_ref, stage_ref):
    days_in = temps_ref.shape[0]
    chunk_rows = span + 1
    stage_ref[0:days_in, :] = temps_ref[...].astype(jnp.float32)
    flags = mask_ref[...].astype(jnp.float32)
    stage_ref[days_in : days_in + 1, :] = flags
    is_flag = lax.broadcasted_iota(jnp.int32, (chunk_rows, out_ref.shape[1]), 0) == span
    for year in range(year_count):
        rows = stage_ref[year * cal_own : year * cal_own + chunk_rows, :]
        tile = jnp.where(is_flag, flags, rows).astype(out_ref.dtype)
        for region in range(region_count):
            first = (region * year_count + year) * chunk_rows
            out_ref[first : first + chunk_rows, :] = tile


def gather_windows(temps, flags, span, cal_own):
    year_count, region_count = lax.axis_size("year"), lax.axis_size("region")
    chunk_rows = span + 1
    lon_own = temps.shape[1]
    rows = pl.pallas_call(
        functools.partial(chunk_kernel, span, cal_own, year_count, region_count),
        out_shape=jax.ShapeDtypeStruct((year_count * region_count * chunk_rows, lon_own), temps.dtype),
        scratch_shapes=[pltpu.VMEM((temps.shape[0] + 1, lon_own), jnp.float32)],
    )(temps, flags.reshape(1, lon_own))
    rows = rows.reshape(year_count * region_count, chunk_rows, lon_own)
    return lax.all_to_all(rows, ("region", "year"), 0, 0, tiled=True)


def coarse_from_samples(samples, count_all, bin_count):
    width = VALUE_RANGE / bin_count
    scaled = jnp.clip((samples + 0.5 * VALUE_RANGE) / width, 0.0, bin_count - 1.0)
    low = count_all * (QUANT_LEVEL - 0.5 / SHARPNESS)
    high = count_all * (QUANT_LEVEL + 0.5 / SHARPNESS)
    block = 8

    def running(points):
        return jnp.sum(jnp.clip(points[None] + 1.0 - scaled[:, None, :], 0.0, 1.0), axis=0)

    ends = lax.broadcasted_iota(jnp.int32, (bin_count // block, 1), 0).astype(jnp.float32) * block + (block - 1)
    at_ends = running(ends)
    full_low = jnp.sum(jnp.where(at_ends <= low, 1.0, 0.0), axis=0)
    full_high = jnp.sum(jnp.where(at_ends < high, 1.0, 0.0), axis=0)
    offsets = lax.broadcasted_iota(jnp.int32, (block, 1), 0).astype(jnp.float32)
    inside = running(jnp.concatenate([full_low[None] * block + offsets, full_high[None] * block + offsets], axis=0))
    first_low = full_low * block + jnp.sum(jnp.where(inside[:block] <= low, 1.0, 0.0), axis=0)
    first_high = full_high * block + jnp.sum(jnp.where(inside[block:] < high, 1.0, 0.0), axis=0)
    between = jnp.sum(jnp.maximum(first_high - scaled, 0.0) - jnp.maximum(first_low - scaled, 0.0), axis=0)
    ranks = first_low + (first_high - first_low) * (0.5 + SHARPNESS * QUANT_LEVEL) - (SHARPNESS / count_all) * between
    return -0.5 * VALUE_RANGE + width * ranks


def shards(daily_temps, land_mask):
    days_in = daily_temps.shape[1]
    lon_own = daily_temps.shape[2]
    year_count = lax.axis_size("year")
    region_count = lax.axis_size("region")
    cal_days = days_in - WIN + 1
    cal_own = cal_days // year_count
    span = WIN + cal_own - 1
    count_all = float(year_count * WIN)
    received = gather_windows(daily_temps[0], land_mask, span, cal_own)
    received = received.reshape(region_count, year_count, span + 1, lon_own)
    region = lax.axis_index("region")
    center = lax.dynamic_index_in_dim(received, region, 0, keepdims=False)
    west = lax.dynamic_index_in_dim(received, lax.rem(region + region_count - 1, region_count), 0, keepdims=False)
    east = lax.dynamic_index_in_dim(received, lax.rem(region + 1, region_count), 0, keepdims=False)
    center = center.astype(jnp.float32)
    to_west = jnp.concatenate([west[..., -1:].astype(jnp.float32), center[..., :-1]], axis=-1)
    to_east = jnp.concatenate([center[..., 1:], east[..., :1].astype(jnp.float32)], axis=-1)
    same_west = 1.0 - jnp.abs(center[0, span] - to_west[0, span])
    same_east = 1.0 - jnp.abs(center[0, span] - to_east[0, span])
    mixed = center[:, :span] + same_west * to_west[:, :span] + same_east * to_east[:, :span]
    every_year = lax.reduce_precision(mixed / (1.0 + same_west + same_east), exponent_bits=8, mantissa_bits=7)
    coarse_rows = []
    refined_rows = []
    for j in range(cal_own):
        samples = every_year[:, j : j + WIN].reshape(-1, lon_own)
        coarse = coarse_from_samples(samples, count_all, BINS)
        cdf = jnp.sum(jax.nn.sigmoid((coarse[None] - samples) / KERNEL_SCALE), axis=0)
        refined = coarse - STEP_SIZE * (cdf / count_all - QUANT_LEVEL)
        coarse_rows.append(coarse)
        refined_rows.append(refined)
    return (jnp.stack(coarse_rows, axis=0), jnp.stack(refined_rows, axis=0))


def solution(mesh):
    return jax.shard_map(
        shards,
        mesh=mesh,
        in_specs=(P("year", None, "region"), P("region")),
        out_specs=(P("year", "region"), P("year", "region")),
        check_vma=False,
    )
```

```python
import functools

import jax
import jax.numpy as jnp
from jax import lax
from jax.experimental import pallas as pl
from jax.experimental.pallas import tpu as pltpu
from jax.sharding import PartitionSpec as P

WIN = 15
BINS = 256


VALUE_RANGE = 12.8
QUANT_LEVEL = 0.9
SHARPNESS = 32.0
KERNEL_SCALE = 0.25
STEP_SIZE = 2.0


def chunk_kernel(span, cal_own, year_count, region_count, temps_hbm, mask_hbm, out_hbm, temps_ref, mask_ref,
                 out_ref, stage_ref, sems):
    loads = [pltpu.make_async_copy(temps_hbm, temps_ref, sems.at[0]), pltpu.make_async_copy(mask_hbm, mask_ref, sems.at[1])]
    for load in loads:
        load.start()
    for load in loads:
        load.wait()
    days_in = temps_ref.shape[0]
    chunk_rows = span + 1
    stage_ref[0:days_in, :] = temps_ref[...].astype(jnp.float32)
    flags = mask_ref[...].astype(jnp.float32)
    stage_ref[days_in : days_in + 1, :] = flags
    is_flag = lax.broadcasted_iota(jnp.int32, (chunk_rows, out_ref.shape[1]), 0) == span
    for year in range(year_count):
        rows = stage_ref[year * cal_own : year * cal_own + chunk_rows, :]
        tile = jnp.where(is_flag, flags, rows).astype(out_ref.dtype)
        for region in range(region_count):
            first = (region * year_count + year) * chunk_rows
            out_ref[first : first + chunk_rows, :] = tile
    store = pltpu.make_async_copy(out_ref, out_hbm, sems.at[2])
    store.start()
    store.wait()


def gather_windows(temps, flags, span, cal_own):
    year_count, region_count = lax.axis_size("year"), lax.axis_size("region")
    chunk_rows = span + 1
    lon_own = temps.shape[1]
    total_rows = year_count * region_count * chunk_rows
    rows = pl.pallas_call(
        functools.partial(chunk_kernel, span, cal_own, year_count, region_count),
        out_shape=jax.ShapeDtypeStruct((total_rows, lon_own), temps.dtype),
        in_specs=[pl.BlockSpec(memory_space=pl.ANY)] * 2,
        out_specs=pl.BlockSpec(memory_space=pl.ANY),
        scratch_shapes=[
            pltpu.VMEM(temps.shape, temps.dtype),
            pltpu.VMEM((1, lon_own), flags.dtype),
            pltpu.VMEM((total_rows, lon_own), temps.dtype),
            pltpu.VMEM((temps.shape[0] + 1, lon_own), jnp.float32),
            pltpu.SemaphoreType.DMA((3,)),
        ],
    )(temps, flags.reshape(1, lon_own))
    rows = rows.reshape(year_count * region_count, chunk_rows, lon_own)
    return lax.all_to_all(rows, ("region", "year"), 0, 0, tiled=True)


def coarse_from_samples(samples, count_all, bin_count):
    width = VALUE_RANGE / bin_count
    scaled = jnp.clip((samples + 0.5 * VALUE_RANGE) / width, 0.0, bin_count - 1.0)
    low = count_all * (QUANT_LEVEL - 0.5 / SHARPNESS)
    high = count_all * (QUANT_LEVEL + 0.5 / SHARPNESS)
    block = 8

    def running(points):
        return jnp.sum(jnp.clip(points[None] + 1.0 - scaled[:, None, :], 0.0, 1.0), axis=0)

    ends = lax.broadcasted_iota(jnp.int32, (bin_count // block, 1), 0).astype(jnp.float32) * block + (block - 1)
    at_ends = running(ends)
    full_low = jnp.sum(jnp.where(at_ends <= low, 1.0, 0.0), axis=0)
    full_high = jnp.sum(jnp.where(at_ends < high, 1.0, 0.0), axis=0)
    offsets = lax.broadcasted_iota(jnp.int32, (block, 1), 0).astype(jnp.float32)
    inside = running(jnp.concatenate([full_low[None] * block + offsets, full_high[None] * block + offsets], axis=0))
    first_low = full_low * block + jnp.sum(jnp.where(inside[:block] <= low, 1.0, 0.0), axis=0)
    first_high = full_high * block + jnp.sum(jnp.where(inside[block:] < high, 1.0, 0.0), axis=0)
    between = jnp.sum(jnp.maximum(first_high - scaled, 0.0) - jnp.maximum(first_low - scaled, 0.0), axis=0)
    ranks = first_low + (first_high - first_low) * (0.5 + SHARPNESS * QUANT_LEVEL) - (SHARPNESS / count_all) * between
    return -0.5 * VALUE_RANGE + width * ranks


def shards(daily_temps, land_mask):
    days_in = daily_temps.shape[1]
    lon_own = daily_temps.shape[2]
    year_count = lax.axis_size("year")
    region_count = lax.axis_size("region")
    cal_days = days_in - WIN + 1
    cal_own = cal_days // year_count
    span = WIN + cal_own - 1
    count_all = float(year_count * WIN)
    received = gather_windows(daily_temps[0], land_mask, span, cal_own)
    received = received.reshape(region_count, year_count, span + 1, lon_own)
    region = lax.axis_index("region")
    center = lax.dynamic_index_in_dim(received, region, 0, keepdims=False)
    west = lax.dynamic_index_in_dim(received, lax.rem(region + region_count - 1, region_count), 0, keepdims=False)
    east = lax.dynamic_index_in_dim(received, lax.rem(region + 1, region_count), 0, keepdims=False)
    center = center.astype(jnp.float32)
    to_west = jnp.concatenate([west[..., -1:].astype(jnp.float32), center[..., :-1]], axis=-1)
    to_east = jnp.concatenate([center[..., 1:], east[..., :1].astype(jnp.float32)], axis=-1)
    same_west = 1.0 - jnp.abs(center[0, span] - to_west[0, span])
    same_east = 1.0 - jnp.abs(center[0, span] - to_east[0, span])
    mixed = center[:, :span] + same_west * to_west[:, :span] + same_east * to_east[:, :span]
    every_year = lax.reduce_precision(mixed / (1.0 + same_west + same_east), exponent_bits=8, mantissa_bits=7)
    coarse_rows = []
    refined_rows = []
    for j in range(cal_own):
        samples = every_year[:, j : j + WIN].reshape(-1, lon_own)
        coarse = coarse_from_samples(samples, count_all, BINS)
        cdf = jnp.sum(jax.nn.sigmoid((coarse[None] - samples) / KERNEL_SCALE), axis=0)
        refined = coarse - STEP_SIZE * (cdf / count_all - QUANT_LEVEL)
        coarse_rows.append(coarse)
        refined_rows.append(refined)
    return (jnp.stack(coarse_rows, axis=0), jnp.stack(refined_rows, axis=0))


def solution(mesh):
    return jax.shard_map(
        shards,
        mesh=mesh,
        in_specs=(P("year", None, "region"), P("region")),
        out_specs=(P("year", "region"), P("year", "region")),
        check_vma=False,
    )
```

```python
import functools

import jax
import jax.numpy as jnp
from jax import lax
from jax.experimental import pallas as pl
from jax.experimental.pallas import tpu as pltpu
from jax.sharding import PartitionSpec as P

WIN = 15
BINS = 256


VALUE_RANGE = 12.8
QUANT_LEVEL = 0.9
SHARPNESS = 32.0
KERNEL_SCALE = 0.25
STEP_SIZE = 2.0


def chunk_kernel(span, cal_own, year_count, region_count, temps_ref, mask_ref, out_ref, stage_ref):
    days_in = temps_ref.shape[0]
    chunk_rows = span + 1
    stage_ref[0:days_in, :] = temps_ref[...].astype(jnp.float32)
    flags = mask_ref[...].astype(jnp.float32)
    stage_ref[days_in : days_in + 1, :] = flags
    is_flag = lax.broadcasted_iota(jnp.int32, (chunk_rows, out_ref.shape[1]), 0) == span
    for year in range(year_count):
        rows = stage_ref[year * cal_own : year * cal_own + chunk_rows, :]
        tile = jnp.where(is_flag, flags, rows).astype(out_ref.dtype)
        for region in range(region_count):
            first = (region * year_count + year) * chunk_rows
            out_ref[first : first + chunk_rows, :] = tile


def gather_windows(temps, flags, span, cal_own):
    year_count, region_count = lax.axis_size("year"), lax.axis_size("region")
    chunk_rows = span + 1
    lon_own = temps.shape[1]
    rows = pl.pallas_call(
        functools.partial(chunk_kernel, span, cal_own, year_count, region_count),
        out_shape=jax.ShapeDtypeStruct((year_count * region_count * chunk_rows, lon_own), temps.dtype),
        scratch_shapes=[pltpu.VMEM((temps.shape[0] + 1, lon_own), jnp.float32)],
    )(temps, flags.reshape(1, lon_own))
    rows = rows.reshape(year_count * region_count, chunk_rows, lon_own)
    return lax.all_to_all(rows, ("region", "year"), 0, 0, tiled=True)


def coarse_from_samples(samples, count_all, bin_count):
    width = VALUE_RANGE / bin_count
    scaled = jnp.clip((samples + 0.5 * VALUE_RANGE) / width, 0.0, bin_count - 1.0)
    low = count_all * (QUANT_LEVEL - 0.5 / SHARPNESS)
    high = count_all * (QUANT_LEVEL + 0.5 / SHARPNESS)

    def running(points):
        return jnp.sum(jnp.clip(points[None] + 1.0 - scaled[:, None, :], 0.0, 1.0), axis=0)

    def counts(values, bound, inclusive):
        return jnp.sum(jnp.where(values <= bound if inclusive else values < bound, 1.0, 0.0), axis=0)

    sizes = (32, 4, 1)
    steps = lax.broadcasted_iota(jnp.int32, (bin_count // sizes[0], 1), 0).astype(jnp.float32)
    at_ends = running(steps * sizes[0] + (sizes[0] - 1))
    first_low = sizes[0] * counts(at_ends, low, True)
    first_high = sizes[0] * counts(at_ends, high, False)
    for parent, size in zip(sizes[:-1], sizes[1:]):
        parts = parent // size
        steps = lax.broadcasted_iota(jnp.int32, (parts, 1), 0).astype(jnp.float32) * size + (size - 1)
        at_ends = running(jnp.concatenate([first_low[None] + steps, first_high[None] + steps], axis=0))
        first_low = first_low + size * counts(at_ends[:parts], low, True)
        first_high = first_high + size * counts(at_ends[parts:], high, False)
    between = jnp.sum(jnp.maximum(first_high - scaled, 0.0) - jnp.maximum(first_low - scaled, 0.0), axis=0)
    ranks = first_low + (first_high - first_low) * (0.5 + SHARPNESS * QUANT_LEVEL) - (SHARPNESS / count_all) * between
    return -0.5 * VALUE_RANGE + width * ranks


def shards(daily_temps, land_mask):
    days_in = daily_temps.shape[1]
    lon_own = daily_temps.shape[2]
    year_count = lax.axis_size("year")
    region_count = lax.axis_size("region")
    cal_days = days_in - WIN + 1
    cal_own = cal_days // year_count
    span = WIN + cal_own - 1
    count_all = float(year_count * WIN)
    received = gather_windows(daily_temps[0], land_mask, span, cal_own)
    received = received.reshape(region_count, year_count, span + 1, lon_own)
    region = lax.axis_index("region")
    center = lax.dynamic_index_in_dim(received, region, 0, keepdims=False)
    west = lax.dynamic_index_in_dim(received, lax.rem(region + region_count - 1, region_count), 0, keepdims=False)
    east = lax.dynamic_index_in_dim(received, lax.rem(region + 1, region_count), 0, keepdims=False)
    center = center.astype(jnp.float32)
    to_west = jnp.concatenate([west[..., -1:].astype(jnp.float32), center[..., :-1]], axis=-1)
    to_east = jnp.concatenate([center[..., 1:], east[..., :1].astype(jnp.float32)], axis=-1)
    same_west = 1.0 - jnp.abs(center[0, span] - to_west[0, span])
    same_east = 1.0 - jnp.abs(center[0, span] - to_east[0, span])
    mixed = center[:, :span] + same_west * to_west[:, :span] + same_east * to_east[:, :span]
    every_year = lax.reduce_precision(mixed / (1.0 + same_west + same_east), exponent_bits=8, mantissa_bits=7)
    coarse_rows = []
    refined_rows = []
    for j in range(cal_own):
        samples = every_year[:, j : j + WIN].reshape(-1, lon_own)
        coarse = coarse_from_samples(samples, count_all, BINS)
        cdf = jnp.sum(jax.nn.sigmoid((coarse[None] - samples) / KERNEL_SCALE), axis=0)
        refined = coarse - STEP_SIZE * (cdf / count_all - QUANT_LEVEL)
        coarse_rows.append(coarse)
        refined_rows.append(refined)
    return (jnp.stack(coarse_rows, axis=0), jnp.stack(refined_rows, axis=0))


def solution(mesh):
    return jax.shard_map(
        shards,
        mesh=mesh,
        in_specs=(P("year", None, "region"), P("region")),
        out_specs=(P("year", "region"), P("year", "region")),
        check_vma=False,
    )
```

```python
import functools

import jax
import jax.numpy as jnp
from jax import lax
from jax.experimental import pallas as pl
from jax.experimental.pallas import tpu as pltpu
from jax.sharding import PartitionSpec as P

WIN = 15
BINS = 256


VALUE_RANGE = 12.8
QUANT_LEVEL = 0.9
SHARPNESS = 32.0
KERNEL_SCALE = 0.25
STEP_SIZE = 2.0


def chunk_kernel(span, cal_own, year_count, region_count, temps_ref, mask_ref, out_ref, stage_ref):
    days_in = temps_ref.shape[0]
    chunk_rows = span + 1
    stage_ref[0:days_in, :] = temps_ref[...].astype(jnp.float32)
    flags = mask_ref[...].astype(jnp.float32)
    stage_ref[days_in : days_in + 1, :] = flags
    is_flag = lax.broadcasted_iota(jnp.int32, (chunk_rows, out_ref.shape[1]), 0) == span
    for year in range(year_count):
        rows = stage_ref[year * cal_own : year * cal_own + chunk_rows, :]
        tile = jnp.where(is_flag, flags, rows).astype(out_ref.dtype)
        for region in range(region_count):
            first = (region * year_count + year) * chunk_rows
            out_ref[first : first + chunk_rows, :] = tile


def gather_windows(temps, flags, span, cal_own):
    year_count, region_count = lax.axis_size("year"), lax.axis_size("region")
    chunk_rows = span + 1
    lon_own = temps.shape[1]
    rows = pl.pallas_call(
        functools.partial(chunk_kernel, span, cal_own, year_count, region_count),
        out_shape=jax.ShapeDtypeStruct((year_count * region_count * chunk_rows, lon_own), temps.dtype),
        scratch_shapes=[pltpu.VMEM((temps.shape[0] + 1, lon_own), jnp.float32)],
    )(temps, flags.reshape(1, lon_own))
    rows = rows.reshape(year_count * region_count, chunk_rows, lon_own)
    return lax.all_to_all(rows, ("region", "year"), 0, 0, tiled=True)


def coarse_from_samples(samples, count_all, bin_count):
    width = VALUE_RANGE / bin_count
    scaled = jnp.clip((samples + 0.5 * VALUE_RANGE) / width, 0.0, bin_count - 1.0)
    low = count_all * (QUANT_LEVEL - 0.5 / SHARPNESS)
    high = count_all * (QUANT_LEVEL + 0.5 / SHARPNESS)
    block = 8

    def running(points):
        return jnp.sum(jnp.clip(points[None] + 1.0 - scaled[:, None, :], 0.0, 1.0), axis=0)

    ends = lax.broadcasted_iota(jnp.int32, (bin_count // block, 1), 0).astype(jnp.float32) * block + (block - 1)
    at_ends = running(ends)
    full_low = jnp.sum(jnp.where(at_ends <= low, 1.0, 0.0), axis=0)
    full_high = jnp.sum(jnp.where(at_ends < high, 1.0, 0.0), axis=0)
    offsets = lax.broadcasted_iota(jnp.int32, (block, 1), 0).astype(jnp.float32)
    inside = running(jnp.concatenate([full_low[None] * block + offsets, full_high[None] * block + offsets], axis=0))
    first_low = full_low * block + jnp.sum(jnp.where(inside[:block] <= low, 1.0, 0.0), axis=0)
    first_high = full_high * block + jnp.sum(jnp.where(inside[block:] < high, 1.0, 0.0), axis=0)
    between = jnp.sum(jnp.maximum(first_high - scaled, 0.0) - jnp.maximum(first_low - scaled, 0.0), axis=0)
    ranks = first_low + (first_high - first_low) * (0.5 + SHARPNESS * QUANT_LEVEL) - (SHARPNESS / count_all) * between
    return -0.5 * VALUE_RANGE + width * ranks


def shards(daily_temps, land_mask):
    days_in = daily_temps.shape[1]
    lon_own = daily_temps.shape[2]
    year_count = lax.axis_size("year")
    region_count = lax.axis_size("region")
    cal_days = days_in - WIN + 1
    cal_own = cal_days // year_count
    span = WIN + cal_own - 1
    count_all = float(year_count * WIN)
    received = gather_windows(daily_temps[0], land_mask, span, cal_own)
    received = received.reshape(region_count, year_count, span + 1, lon_own)
    region = lax.axis_index("region")
    center = lax.dynamic_index_in_dim(received, region, 0, keepdims=False)
    west = lax.dynamic_index_in_dim(received, lax.rem(region + region_count - 1, region_count), 0, keepdims=False)
    east = lax.dynamic_index_in_dim(received, lax.rem(region + 1, region_count), 0, keepdims=False)
    center = center.astype(jnp.float32)
    to_west = jnp.concatenate([west[..., -1:].astype(jnp.float32), center[..., :-1]], axis=-1)
    to_east = jnp.concatenate([center[..., 1:], east[..., :1].astype(jnp.float32)], axis=-1)
    flags = land_mask.astype(jnp.float32)
    flag_west = jnp.concatenate([west[0, span, -1:].astype(jnp.float32), flags[:-1]])
    flag_east = jnp.concatenate([flags[1:], east[0, span, :1].astype(jnp.float32)])
    same_west = 1.0 - jnp.abs(flags - flag_west)
    same_east = 1.0 - jnp.abs(flags - flag_east)
    mixed = center[:, :span] + same_west * to_west[:, :span] + same_east * to_east[:, :span]
    every_year = lax.reduce_precision(mixed / (1.0 + same_west + same_east), exponent_bits=8, mantissa_bits=7)
    coarse_rows = []
    refined_rows = []
    for j in range(cal_own):
        samples = every_year[:, j : j + WIN].reshape(-1, lon_own)
        coarse = coarse_from_samples(samples, count_all, BINS)
        cdf = jnp.sum(jax.nn.sigmoid((coarse[None] - samples) / KERNEL_SCALE), axis=0)
        refined = coarse - STEP_SIZE * (cdf / count_all - QUANT_LEVEL)
        coarse_rows.append(coarse)
        refined_rows.append(refined)
    return (jnp.stack(coarse_rows, axis=0), jnp.stack(refined_rows, axis=0))


def solution(mesh):
    return jax.shard_map(
        shards,
        mesh=mesh,
        in_specs=(P("year", None, "region"), P("region")),
        out_specs=(P("year", "region"), P("year", "region")),
        check_vma=False,
    )
```

```python
import functools

import jax
import jax.numpy as jnp
from jax import lax
from jax.experimental import pallas as pl
from jax.experimental.pallas import tpu as pltpu
from jax.sharding import PartitionSpec as P

WIN = 15
BINS = 256


VALUE_RANGE = 12.8
QUANT_LEVEL = 0.9
SHARPNESS = 32.0
KERNEL_SCALE = 0.25
STEP_SIZE = 2.0


def chunk_kernel(span, cal_own, year_count, region_count, temps_ref, mask_ref, out_ref, stage_ref):
    days_in = temps_ref.shape[0]
    chunk_rows = span + 1
    stage_ref[0:days_in, :] = temps_ref[...].astype(jnp.float32)
    flags = mask_ref[...].astype(jnp.float32)
    stage_ref[days_in : days_in + 1, :] = flags
    is_flag = lax.broadcasted_iota(jnp.int32, (chunk_rows, out_ref.shape[1]), 0) == span
    for year in range(year_count):
        rows = stage_ref[year * cal_own : year * cal_own + chunk_rows, :]
        tile = jnp.where(is_flag, flags, rows).astype(out_ref.dtype)
        for region in range(region_count):
            first = (region * year_count + year) * chunk_rows
            out_ref[first : first + chunk_rows, :] = tile


def gather_windows(temps, flags, span, cal_own):
    year_count, region_count = lax.axis_size("year"), lax.axis_size("region")
    chunk_rows = span + 1
    lon_own = temps.shape[1]
    rows = pl.pallas_call(
        functools.partial(chunk_kernel, span, cal_own, year_count, region_count),
        out_shape=jax.ShapeDtypeStruct((year_count * region_count * chunk_rows, lon_own), temps.dtype),
        scratch_shapes=[pltpu.VMEM((temps.shape[0] + 1, lon_own), jnp.float32)],
    )(temps, flags.reshape(1, lon_own))
    rows = rows.reshape(year_count * region_count, chunk_rows, lon_own)
    return lax.all_to_all(rows, ("region", "year"), 0, 0, tiled=True)


def coarse_from_samples(samples, count_all, bin_count):
    width = VALUE_RANGE / bin_count
    scaled = jnp.clip((samples + 0.5 * VALUE_RANGE) / width, 0.0, bin_count - 1.0)
    low = count_all * (QUANT_LEVEL - 0.5 / SHARPNESS)
    high = count_all * (QUANT_LEVEL + 0.5 / SHARPNESS)
    block = 16

    def running(points):
        return jnp.sum(jnp.clip(points[None] + 1.0 - scaled[:, None, :], 0.0, 1.0), axis=0)

    ends = lax.broadcasted_iota(jnp.int32, (bin_count // block, 1), 0).astype(jnp.float32) * block + (block - 1)
    at_ends = running(ends)
    full_low = jnp.sum(jnp.where(at_ends <= low, 1.0, 0.0), axis=0)
    full_high = jnp.sum(jnp.where(at_ends < high, 1.0, 0.0), axis=0)
    offsets = lax.broadcasted_iota(jnp.int32, (block, 1), 0).astype(jnp.float32)
    inside = running(jnp.concatenate([full_low[None] * block + offsets, full_high[None] * block + offsets], axis=0))
    first_low = full_low * block + jnp.sum(jnp.where(inside[:block] <= low, 1.0, 0.0), axis=0)
    first_high = full_high * block + jnp.sum(jnp.where(inside[block:] < high, 1.0, 0.0), axis=0)
    between = jnp.sum(jnp.maximum(first_high - scaled, 0.0) - jnp.maximum(first_low - scaled, 0.0), axis=0)
    ranks = first_low + (first_high - first_low) * (0.5 + SHARPNESS * QUANT_LEVEL) - (SHARPNESS / count_all) * between
    return -0.5 * VALUE_RANGE + width * ranks


def shards(daily_temps, land_mask):
    days_in = daily_temps.shape[1]
    lon_own = daily_temps.shape[2]
    year_count = lax.axis_size("year")
    region_count = lax.axis_size("region")
    cal_days = days_in - WIN + 1
    cal_own = cal_days // year_count
    span = WIN + cal_own - 1
    count_all = float(year_count * WIN)
    received = gather_windows(daily_temps[0], land_mask, span, cal_own)
    received = received.reshape(region_count, year_count, span + 1, lon_own)
    region = lax.axis_index("region")
    center = lax.dynamic_index_in_dim(received, region, 0, keepdims=False)
    west = lax.dynamic_index_in_dim(received, lax.rem(region + region_count - 1, region_count), 0, keepdims=False)
    east = lax.dynamic_index_in_dim(received, lax.rem(region + 1, region_count), 0, keepdims=False)
    center = center.astype(jnp.float32)
    to_west = jnp.concatenate([west[..., -1:].astype(jnp.float32), center[..., :-1]], axis=-1)
    to_east = jnp.concatenate([center[..., 1:], east[..., :1].astype(jnp.float32)], axis=-1)
    same_west = 1.0 - jnp.abs(center[0, span] - to_west[0, span])
    same_east = 1.0 - jnp.abs(center[0, span] - to_east[0, span])
    mixed = center[:, :span] + same_west * to_west[:, :span] + same_east * to_east[:, :span]
    every_year = lax.reduce_precision(mixed / (1.0 + same_west + same_east), exponent_bits=8, mantissa_bits=7)
    coarse_rows = []
    refined_rows = []
    for j in range(cal_own):
        samples = every_year[:, j : j + WIN].reshape(-1, lon_own)
        coarse = coarse_from_samples(samples, count_all, BINS)
        cdf = jnp.sum(jax.nn.sigmoid((coarse[None] - samples) / KERNEL_SCALE), axis=0)
        refined = coarse - STEP_SIZE * (cdf / count_all - QUANT_LEVEL)
        coarse_rows.append(coarse)
        refined_rows.append(refined)
    return (jnp.stack(coarse_rows, axis=0), jnp.stack(refined_rows, axis=0))


def solution(mesh):
    return jax.shard_map(
        shards,
        mesh=mesh,
        in_specs=(P("year", None, "region"), P("region")),
        out_specs=(P("year", "region"), P("year", "region")),
        check_vma=False,
    )
```

```python
import functools

import jax
import jax.numpy as jnp
from jax import lax
from jax.experimental import pallas as pl
from jax.experimental.pallas import tpu as pltpu
from jax.sharding import PartitionSpec as P

WIN = 15
BINS = 256


VALUE_RANGE = 12.8
QUANT_LEVEL = 0.9
SHARPNESS = 32.0
KERNEL_SCALE = 0.25
STEP_SIZE = 2.0


def chunk_kernel(span, cal_own, year_count, region_count, temps_ref, mask_ref, out_ref, stage_ref):
    days_in = temps_ref.shape[0]
    chunk_rows = span + 1
    stage_ref[0:days_in, :] = temps_ref[...].astype(jnp.float32)
    flags = mask_ref[...].astype(jnp.float32)
    stage_ref[days_in : days_in + 1, :] = flags
    is_flag = lax.broadcasted_iota(jnp.int32, (chunk_rows, out_ref.shape[1]), 0) == span
    for year in range(year_count):
        rows = stage_ref[year * cal_own : year * cal_own + chunk_rows, :]
        tile = jnp.where(is_flag, flags, rows).astype(out_ref.dtype)
        for region in range(region_count):
            first = (year * region_count + region) * chunk_rows
            out_ref[first : first + chunk_rows, :] = tile


def gather_windows(temps, flags, span, cal_own):
    year_count, region_count = lax.axis_size("year"), lax.axis_size("region")
    chunk_rows = span + 1
    lon_own = temps.shape[1]
    rows = pl.pallas_call(
        functools.partial(chunk_kernel, span, cal_own, year_count, region_count),
        out_shape=jax.ShapeDtypeStruct((year_count * region_count * chunk_rows, lon_own), temps.dtype),
        scratch_shapes=[pltpu.VMEM((temps.shape[0] + 1, lon_own), jnp.float32)],
    )(temps, flags.reshape(1, lon_own))
    rows = rows.reshape(year_count * region_count, chunk_rows, lon_own)
    return lax.all_to_all(rows, ("year", "region"), 0, 0, tiled=True)


def coarse_from_samples(samples, count_all, bin_count):
    width = VALUE_RANGE / bin_count
    scaled = jnp.clip((samples + 0.5 * VALUE_RANGE) / width, 0.0, bin_count - 1.0)
    low = count_all * (QUANT_LEVEL - 0.5 / SHARPNESS)
    high = count_all * (QUANT_LEVEL + 0.5 / SHARPNESS)
    block = 8

    def running(points):
        return jnp.sum(jnp.clip(points[None] + 1.0 - scaled[:, None, :], 0.0, 1.0), axis=0)

    ends = lax.broadcasted_iota(jnp.int32, (bin_count // block, 1), 0).astype(jnp.float32) * block + (block - 1)
    at_ends = running(ends)
    full_low = jnp.sum(jnp.where(at_ends <= low, 1.0, 0.0), axis=0)
    full_high = jnp.sum(jnp.where(at_ends < high, 1.0, 0.0), axis=0)
    offsets = lax.broadcasted_iota(jnp.int32, (block, 1), 0).astype(jnp.float32)
    inside = running(jnp.concatenate([full_low[None] * block + offsets, full_high[None] * block + offsets], axis=0))
    first_low = full_low * block + jnp.sum(jnp.where(inside[:block] <= low, 1.0, 0.0), axis=0)
    first_high = full_high * block + jnp.sum(jnp.where(inside[block:] < high, 1.0, 0.0), axis=0)
    between = jnp.sum(jnp.maximum(first_high - scaled, 0.0) - jnp.maximum(first_low - scaled, 0.0), axis=0)
    ranks = first_low + (first_high - first_low) * (0.5 + SHARPNESS * QUANT_LEVEL) - (SHARPNESS / count_all) * between
    return -0.5 * VALUE_RANGE + width * ranks


def shards(daily_temps, land_mask):
    days_in = daily_temps.shape[1]
    lon_own = daily_temps.shape[2]
    year_count = lax.axis_size("year")
    region_count = lax.axis_size("region")
    cal_days = days_in - WIN + 1
    cal_own = cal_days // year_count
    span = WIN + cal_own - 1
    count_all = float(year_count * WIN)
    received = gather_windows(daily_temps[0], land_mask, span, cal_own)
    received = jnp.swapaxes(received.reshape(year_count, region_count, span + 1, lon_own), 0, 1)
    region = lax.axis_index("region")
    center = lax.dynamic_index_in_dim(received, region, 0, keepdims=False)
    west = lax.dynamic_index_in_dim(received, lax.rem(region + region_count - 1, region_count), 0, keepdims=False)
    east = lax.dynamic_index_in_dim(received, lax.rem(region + 1, region_count), 0, keepdims=False)
    center = center.astype(jnp.float32)
    to_west = jnp.concatenate([west[..., -1:].astype(jnp.float32), center[..., :-1]], axis=-1)
    to_east = jnp.concatenate([center[..., 1:], east[..., :1].astype(jnp.float32)], axis=-1)
    same_west = 1.0 - jnp.abs(center[0, span] - to_west[0, span])
    same_east = 1.0 - jnp.abs(center[0, span] - to_east[0, span])
    mixed = center[:, :span] + same_west * to_west[:, :span] + same_east * to_east[:, :span]
    every_year = lax.reduce_precision(mixed / (1.0 + same_west + same_east), exponent_bits=8, mantissa_bits=7)
    coarse_rows = []
    refined_rows = []
    for j in range(cal_own):
        samples = every_year[:, j : j + WIN].reshape(-1, lon_own)
        coarse = coarse_from_samples(samples, count_all, BINS)
        cdf = jnp.sum(jax.nn.sigmoid((coarse[None] - samples) / KERNEL_SCALE), axis=0)
        refined = coarse - STEP_SIZE * (cdf / count_all - QUANT_LEVEL)
        coarse_rows.append(coarse)
        refined_rows.append(refined)
    return (jnp.stack(coarse_rows, axis=0), jnp.stack(refined_rows, axis=0))


def solution(mesh):
    return jax.shard_map(
        shards,
        mesh=mesh,
        in_specs=(P("year", None, "region"), P("region")),
        out_specs=(P("year", "region"), P("year", "region")),
        check_vma=False,
    )
```

```python
import functools

import jax
import jax.numpy as jnp
from jax import lax
from jax.experimental import pallas as pl
from jax.experimental.pallas import tpu as pltpu
from jax.sharding import PartitionSpec as P

WIN = 15
BINS = 256


VALUE_RANGE = 12.8
QUANT_LEVEL = 0.9
SHARPNESS = 32.0
KERNEL_SCALE = 0.25
STEP_SIZE = 2.0


def chunk_kernel(span, cal_own, year_count, region_count, temps_ref, mask_ref, out_hbm, stage_ref, tiles_ref, sems):
    days_in = temps_ref.shape[0]
    chunk_rows = span + 1
    stage_ref[0:days_in, :] = temps_ref[...].astype(jnp.float32)
    flags = mask_ref[...].astype(jnp.float32)
    stage_ref[days_in : days_in + 1, :] = flags
    is_flag = lax.broadcasted_iota(jnp.int32, (chunk_rows, tiles_ref.shape[2]), 0) == span
    copies = []
    for year in range(year_count):
        rows = stage_ref[year * cal_own : year * cal_own + chunk_rows, :]
        tiles_ref[year] = jnp.where(is_flag, flags, rows).astype(tiles_ref.dtype)
        for region in range(region_count):
            first = (region * year_count + year) * chunk_rows
            copy = pltpu.make_async_copy(
                tiles_ref.at[year], out_hbm.at[pl.ds(first, chunk_rows)], sems.at[year * region_count + region]
            )
            copy.start()
            copies.append(copy)
    for copy in copies:
        copy.wait()


def gather_windows(temps, flags, span, cal_own):
    year_count, region_count = lax.axis_size("year"), lax.axis_size("region")
    chunk_rows = span + 1
    lon_own = temps.shape[1]
    rows = pl.pallas_call(
        functools.partial(chunk_kernel, span, cal_own, year_count, region_count),
        out_shape=jax.ShapeDtypeStruct((year_count * region_count * chunk_rows, lon_own), temps.dtype),
        out_specs=pl.BlockSpec(memory_space=pl.ANY),
        scratch_shapes=[
            pltpu.VMEM((temps.shape[0] + 1, lon_own), jnp.float32),
            pltpu.VMEM((year_count, chunk_rows, lon_own), temps.dtype),
            pltpu.SemaphoreType.DMA((year_count * region_count,)),
        ],
    )(temps, flags.reshape(1, lon_own))
    rows = rows.reshape(year_count * region_count, chunk_rows, lon_own)
    return lax.all_to_all(rows, ("region", "year"), 0, 0, tiled=True)


def coarse_from_samples(samples, count_all, bin_count):
    width = VALUE_RANGE / bin_count
    scaled = jnp.clip((samples + 0.5 * VALUE_RANGE) / width, 0.0, bin_count - 1.0)
    low = count_all * (QUANT_LEVEL - 0.5 / SHARPNESS)
    high = count_all * (QUANT_LEVEL + 0.5 / SHARPNESS)
    block = 8

    def running(points):
        return jnp.sum(jnp.clip(points[None] + 1.0 - scaled[:, None, :], 0.0, 1.0), axis=0)

    ends = lax.broadcasted_iota(jnp.int32, (bin_count // block, 1), 0).astype(jnp.float32) * block + (block - 1)
    at_ends = running(ends)
    full_low = jnp.sum(jnp.where(at_ends <= low, 1.0, 0.0), axis=0)
    full_high = jnp.sum(jnp.where(at_ends < high, 1.0, 0.0), axis=0)
    offsets = lax.broadcasted_iota(jnp.int32, (block, 1), 0).astype(jnp.float32)
    inside = running(jnp.concatenate([full_low[None] * block + offsets, full_high[None] * block + offsets], axis=0))
    first_low = full_low * block + jnp.sum(jnp.where(inside[:block] <= low, 1.0, 0.0), axis=0)
    first_high = full_high * block + jnp.sum(jnp.where(inside[block:] < high, 1.0, 0.0), axis=0)
    between = jnp.sum(jnp.maximum(first_high - scaled, 0.0) - jnp.maximum(first_low - scaled, 0.0), axis=0)
    ranks = first_low + (first_high - first_low) * (0.5 + SHARPNESS * QUANT_LEVEL) - (SHARPNESS / count_all) * between
    return -0.5 * VALUE_RANGE + width * ranks


def shards(daily_temps, land_mask):
    days_in = daily_temps.shape[1]
    lon_own = daily_temps.shape[2]
    year_count = lax.axis_size("year")
    region_count = lax.axis_size("region")
    cal_days = days_in - WIN + 1
    cal_own = cal_days // year_count
    span = WIN + cal_own - 1
    count_all = float(year_count * WIN)
    received = gather_windows(daily_temps[0], land_mask, span, cal_own)
    received = received.reshape(region_count, year_count, span + 1, lon_own)
    region = lax.axis_index("region")
    center = lax.dynamic_index_in_dim(received, region, 0, keepdims=False)
    west = lax.dynamic_index_in_dim(received, lax.rem(region + region_count - 1, region_count), 0, keepdims=False)
    east = lax.dynamic_index_in_dim(received, lax.rem(region + 1, region_count), 0, keepdims=False)
    center = center.astype(jnp.float32)
    to_west = jnp.concatenate([west[..., -1:].astype(jnp.float32), center[..., :-1]], axis=-1)
    to_east = jnp.concatenate([center[..., 1:], east[..., :1].astype(jnp.float32)], axis=-1)
    same_west = 1.0 - jnp.abs(center[0, span] - to_west[0, span])
    same_east = 1.0 - jnp.abs(center[0, span] - to_east[0, span])
    mixed = center[:, :span] + same_west * to_west[:, :span] + same_east * to_east[:, :span]
    every_year = lax.reduce_precision(mixed / (1.0 + same_west + same_east), exponent_bits=8, mantissa_bits=7)
    coarse_rows = []
    refined_rows = []
    for j in range(cal_own):
        samples = every_year[:, j : j + WIN].reshape(-1, lon_own)
        coarse = coarse_from_samples(samples, count_all, BINS)
        cdf = jnp.sum(jax.nn.sigmoid((coarse[None] - samples) / KERNEL_SCALE), axis=0)
        refined = coarse - STEP_SIZE * (cdf / count_all - QUANT_LEVEL)
        coarse_rows.append(coarse)
        refined_rows.append(refined)
    return (jnp.stack(coarse_rows, axis=0), jnp.stack(refined_rows, axis=0))


def solution(mesh):
    return jax.shard_map(
        shards,
        mesh=mesh,
        in_specs=(P("year", None, "region"), P("region")),
        out_specs=(P("year", "region"), P("year", "region")),
        check_vma=False,
    )
```
